32 devices in a mesh: groups: 2 (over y), spec: 8 (over z, core), lat: 2 (over x).
Axes of the slice: x: 2, y: 2, z: 4, core: 2. Of those that a mesh axis runs over, the one named last changes fastest.
Arguments:
- spectrum: float32 [1152, 64, 256], P('spec', 'lat', 'groups'), parts along dimension 2, may hold values from 0.05 to 1
- transparency: float32 [64, 256], P('lat', 'groups'), parts along dimension 1, may hold values from 0 to 1, as said below
- sea_order: int32 [64, 256], P('lat', 'groups'), parts along dimension 1, may hold values from 0 to 4095, as said below
- speeds: float32 [32], replicated, may hold values from 0.15 to 0.9
- sprinkle: float32 [32], replicated, may hold values from 0.04 to 0.25
- coupling: float32 [32], replicated, may hold values from 0.3 to 3
- quad_offsets: int32 [4], replicated, may hold values from 1 to 4, as said below
Outputs:
- updated: float32 [1152, 64, 256], P('spec', 'lat', 'groups'), parts along dimension 2
- source: bfloat16 [4, 1152, 3072], P(('groups', 'lat'), None, 'spec'), parts along dimension 0
The draws below stay inside these ranges and needn't reach their ends.
There are 2 independent parts, one for each index of `groups`. The reference program is written for one: setup_inputs(seed, part) draws one part's arguments, and reference() takes and returns one part's arrays. A program takes and returns all parts, laid end to end along the dimension named above; an argument that names none is the same for every part. Nothing has to cross between parts.
Inputs may be any that keep to these rules, and one draw needn't show every extreme that they name: Every band of 32 rows holds at most 3072 cells of positive transparency (sea cells), and some band exactly 3072; land cells are exactly 0. `sea_order`: read row by row, each band of 32 rows holds a permutation of its row-major cell positions, all sea cells first. `quad_offsets`: bins up and down in frequency, then direction bins of the first and second partner.
All inputs are finite; a program needn't handle non-finite values.
Results may differ from the reference program's by a relative error of at most 0.001.
Values sent between devices are 32-bit elements; how exact they have to be, the bound alone decides.
No kernel may reach another device: no remote copies, remote signals or barrier semaphores. Data moves between devices by JAX's collectives and lax.ppermute only.
A program may use at most 64 MiB of HBM per device.

```python
import math
import jax
import jax.numpy as jnp
from jax import lax

NDIR = 36
NFREQ = 32
ROWS_DEV = 32
X = 128
SUBSTEPS = 2
COMPONENTS = 1152
BANDS = 2
Y = 64
SEA_MAX = 3072


def sea_layout(key):
    count_key = jax.random.fold_in(key, 101)
    pick_key = jax.random.fold_in(key, 102)
    perm_key = jax.random.fold_in(key, 103)
    cells = ROWS_DEV * X
    counts = jax.random.randint(count_key, (BANDS,), SEA_MAX // 2, SEA_MAX + 1)
    chosen = jax.random.randint(pick_key, (), 0, BANDS)
    counts = jnp.where(lax.iota(jnp.int32, BANDS) == chosen, SEA_MAX, counts)

    def shuffled(band_key):
        return jax.random.permutation(band_key, cells).astype(jnp.int32)
    ranks = jax.vmap(shuffled)(jax.random.split(perm_key, BANDS))
    is_sea = ranks < counts[:, None]
    sort_keys = jnp.where(is_sea, ranks, ranks + cells)
    ordering = jnp.argsort(sort_keys, axis=1, stable=True).astype(jnp.int32)
    return (is_sea.astype(jnp.int32).reshape(Y, X), ordering.reshape(Y, X))


def draw_transparency(key, part):
    is_sea = sea_layout(key)[0]
    level_key = jax.random.fold_in(key, 301)
    levels = jax.random.uniform(level_key, (Y, X), jnp.float32, 0.6, 1.0)
    return is_sea.astype(jnp.float32) * levels


def draw_sea_order(key, part):
    return sea_layout(key)[1]


def draw_quad_offsets(key, part):
    up_freq = jax.random.randint(jax.random.fold_in(key, 201), (), 2, 4)
    dir_two = jax.random.randint(jax.random.fold_in(key, 202), (), 2, 4)
    return jnp.stack([up_freq, jnp.int32(4), jnp.int32(1), dir_two]).astype(jnp.int32)


def shard_levels(own_key, extent, cuts, least, largest):
    def one(dim, shards_of):
        heights = jax.random.uniform(jax.random.fold_in(jax.random.fold_in(own_key, 6), dim), (shards_of,), jnp.float32, least / len(cuts), largest / len(cuts))
        return jnp.repeat(jnp.exp(heights), extent[dim] // shards_of).reshape((-1,) + (1,) * (len(extent) - dim - 1))

    loudness = one(*cuts[0])
    for cut in cuts[1:]:
        loudness = loudness * one(*cut)
    return loudness


def setup_inputs(seed: int = 0, part: int = 0) -> dict:
    key_list = jax.random.split(jax.random.key(seed), 8)
    part_splits = jax.random.split(jax.random.fold_in(key_list[7], part), 8)
    return {
        "spectrum": jnp.clip(jnp.exp(math.log(1.0) - 2.9957323 * jax.random.uniform(part_splits[0], (COMPONENTS, Y, X), jnp.float32) ** shard_levels(part_splits[0], (COMPONENTS, Y, X), ((0, 8), (1, 2)), -0.2, 0.2)), 0.05, 1.0),
        "transparency": draw_transparency(jax.random.fold_in(jax.random.fold_in(key_list[7], part), 71), part),
        "sea_order": draw_sea_order(jax.random.fold_in(jax.random.fold_in(key_list[7], part), 71), part),
        "speeds": jnp.clip(jnp.exp(jax.random.uniform(key_list[3], (NFREQ,), jnp.float32, math.log(0.15), math.log(0.9))), 0.15, 0.9),
        "sprinkle": jnp.clip(jnp.exp(jax.random.uniform(key_list[4], (NFREQ,), jnp.float32, math.log(0.04), math.log(0.25))), 0.04, 0.25),
        "coupling": jnp.clip(jnp.exp(jax.random.uniform(key_list[5], (NFREQ,), jnp.float32, math.log(0.3), math.log(3.0))), 0.3, 3.0),
        "quad_offsets": draw_quad_offsets(jax.random.fold_in(key_list[7], 71), part),
    }


gain_up = 1.25 ** -4
gain_down = 0.75 ** -4
gain_cross = 0.9375 ** -4


def cut_slab(values, offset, length, along):
    return lax.slice_in_dim(values, offset, offset + length, axis=along)


def pad_along(values, along):
    if along == 1:
        return jnp.pad(values, ((0, 0), (2, 2), (0, 0)))
    return jnp.pad(values, ((0, 0), (0, 0), (2, 2)))


def quickest(padded, courant, along):
    length = padded.shape[along] - 4
    before_cell = cut_slab(padded, 0, length + 1, along)
    left_cell = cut_slab(padded, 1, length + 1, along)
    right_cell = cut_slab(padded, 2, length + 1, along)
    after_cell = cut_slab(padded, 3, length + 1, along)
    curvature = jnp.where(courant > 0, right_cell - 2.0 * left_cell + before_cell, after_cell - 2.0 * right_cell + left_cell)
    face_value = 0.5 * (left_cell + right_cell) - 0.5 * courant * (right_cell - left_cell) - (1.0 - courant * courant) / 6.0 * curvature
    face_flux = courant * face_value
    return cut_slab(padded, 2, length, along) - (cut_slab(face_flux, 1, length, along) - cut_slab(face_flux, 0, length, along))


def laplace(padded, along):
    length = padded.shape[along] - 4
    centre = cut_slab(padded, 2, length, along)
    near_sum = cut_slab(padded, 1, length, along) + cut_slab(padded, 3, length, along) - 2.0 * centre
    far_sum = cut_slab(padded, 0, length, along) + cut_slab(padded, 4, length, along) - 2.0 * centre
    return (4.0 / 3.0) * near_sum - (1.0 / 12.0) * far_sum


def interact(columns, coupling, quad_offsets):
    initial = columns.shape
    spectra = columns.reshape(NFREQ, NDIR, -1)
    up_freq = quad_offsets[0]
    down_freq = quad_offsets[1]
    dir_one = quad_offsets[2]
    dir_two = quad_offsets[3]
    freq_index = lax.iota(jnp.int32, NFREQ)[:, None, None]
    inside = ((freq_index + up_freq < NFREQ) & (freq_index - down_freq >= 0)).astype(jnp.float32)
    weight = coupling[:, None, None] * inside
    source_sum = jnp.zeros_like(spectra)
    for mirror in (1, -1):
        upper_bin = jnp.roll(jnp.roll(spectra, -up_freq, 0), -mirror * dir_one, 1)
        lower_bin = jnp.roll(jnp.roll(spectra, down_freq, 0), mirror * dir_two, 1)
        squared = spectra * spectra
        transfer = weight * (squared * (upper_bin * gain_up + lower_bin * gain_down) - 2.0 * gain_cross * spectra * upper_bin * lower_bin)
        source_sum = source_sum - 2.0 * transfer
        source_sum = source_sum + jnp.roll(jnp.roll(transfer, up_freq, 0), mirror * dir_one, 1)
        source_sum = source_sum + jnp.roll(jnp.roll(transfer, -down_freq, 0), -mirror * dir_two, 1)
    return source_sum.reshape(initial)


def reference(spectrum, transparency, sea_order, speeds, sprinkle, coupling, quad_offsets):
    sea_mask = transparency
    angles = 2.0 * math.pi * (lax.iota(jnp.int32, NDIR).astype(jnp.float32) + 0.5) / NDIR
    sines = jnp.sin(angles)
    cosines = jnp.cos(angles)

    def propagate_freq(inputs):
        freq_block, speed_one, spread = inputs
        courant_y = (speed_one * sines)[:, None, None]
        courant_x = (speed_one * cosines)[:, None, None]
        energy = freq_block.astype(jnp.float32)
        for substep in range(SUBSTEPS):
            energy = quickest(pad_along(energy, 1), courant_y, 1)
            energy = quickest(pad_along(energy, 2), courant_x, 2) * sea_mask
        spread_y = (spread * (sines * sines + 0.25 * cosines * cosines))[:, None, None]
        spread_x = (spread * (cosines * cosines + 0.25 * sines * sines))[:, None, None]
        return (energy + spread_y * laplace(pad_along(energy, 1), 1) + spread_x * laplace(pad_along(energy, 2), 2)) * sea_mask

    smoothed = lax.map(propagate_freq, (spectrum.reshape(NFREQ, NDIR, Y, X), speeds, sprinkle))
    band_cells = smoothed.reshape(COMPONENTS, BANDS, ROWS_DEV * X)
    orders = sea_order.reshape(BANDS, ROWS_DEV * X)

    def one_band(band_index):
        band = lax.dynamic_slice_in_dim(band_cells, band_index, 1, 1)[:, 0, :]
        sea_cells = lax.dynamic_slice_in_dim(orders, band_index, 1, 0)[0, :SEA_MAX]
        columns = jnp.take(band, sea_cells, axis=1)
        source_terms = interact(columns, coupling, quad_offsets)
        return band.at[:, sea_cells].add(source_terms), source_terms.astype(jnp.bfloat16)

    new_bands, source = lax.map(one_band, lax.iota(jnp.int32, BANDS))
    updated = jnp.transpose(new_bands, (1, 0, 2)).reshape(COMPONENTS, Y, X)
    return updated, source
```

```python
import math

import jax
import jax.numpy as jnp
from jax import lax
from jax.sharding import PartitionSpec as P

NDIR = 36
NFREQ = 32
SUBSTEPS = 2
SEA_MAX = 3072
CHUNKS = 2


gain_up = 1.25 ** (-4)
gain_down = 0.75 ** (-4)
gain_cross = 0.9375 ** (-4)


def extended_2(block, sides, width):
    for axis, dim in sides:
        count = lax.axis_size(axis)
        forward = [(i, i + 1) for i in range(count - 1)]
        backward = [(target, source) for source, target in forward]
        low = lax.ppermute(
            lax.slice_in_dim(block, block.shape[dim] - width, None, axis=dim), axis, forward
        )
        high = lax.ppermute(lax.slice_in_dim(block, 0, width, axis=dim), axis, backward)
        block = jnp.concatenate([low, block, high], axis=dim)
    return block


def cut_slab(values, offset, length, along):
    return lax.slice_in_dim(values, offset, offset + length, axis=along)


def pad_along(values):
    return jnp.pad(values, ((0, 0), (0, 0), (2, 2)))


def quickest(padded, courant, along):
    length = padded.shape[along] - 4
    before_cell = cut_slab(padded, 0, length + 1, along)
    left_cell = cut_slab(padded, 1, length + 1, along)
    right_cell = cut_slab(padded, 2, length + 1, along)
    after_cell = cut_slab(padded, 3, length + 1, along)
    curvature = jnp.where(
        courant > 0,
        right_cell - 2.0 * left_cell + before_cell,
        after_cell - 2.0 * right_cell + left_cell,
    )
    face_value = (
        0.5 * (left_cell + right_cell)
        - 0.5 * courant * (right_cell - left_cell)
        - (1.0 - courant * courant) / 6.0 * curvature
    )
    face_flux = courant * face_value
    return cut_slab(padded, 2, length, along) - (
        cut_slab(face_flux, 1, length, along) - cut_slab(face_flux, 0, length, along)
    )


def laplace(padded, along):
    length = padded.shape[along] - 4
    centre = cut_slab(padded, 2, length, along)
    near_sum = (
        cut_slab(padded, 1, length, along) + cut_slab(padded, 3, length, along) - 2.0 * centre
    )
    far_sum = cut_slab(padded, 0, length, along) + cut_slab(padded, 4, length, along) - 2.0 * centre
    return 4.0 / 3.0 * near_sum - 1.0 / 12.0 * far_sum


def interact(columns, coupling, quad_offsets):
    initial = columns.shape
    spectra = columns.reshape(NFREQ, NDIR, -1)
    up_freq = quad_offsets[0]
    down_freq = quad_offsets[1]
    dir_one = quad_offsets[2]
    dir_two = quad_offsets[3]
    freq_index = lax.iota(jnp.int32, NFREQ)[:, None, None]
    inside = ((freq_index + up_freq < NFREQ) & (freq_index - down_freq >= 0)).astype(jnp.float32)
    weight = coupling[:, None, None] * inside
    source_sum = jnp.zeros_like(spectra)
    for mirror in (1, -1):
        upper_bin = jnp.roll(jnp.roll(spectra, -up_freq, 0), -mirror * dir_one, 1)
        lower_bin = jnp.roll(jnp.roll(spectra, down_freq, 0), mirror * dir_two, 1)
        squared = spectra * spectra
        transfer = weight * (
            squared * (upper_bin * gain_up + lower_bin * gain_down)
            - 2.0 * gain_cross * spectra * upper_bin * lower_bin
        )
        source_sum = source_sum - 2.0 * transfer
        source_sum = source_sum + jnp.roll(jnp.roll(transfer, up_freq, 0), mirror * dir_one, 1)
        source_sum = source_sum + jnp.roll(jnp.roll(transfer, -down_freq, 0), -mirror * dir_two, 1)
    return source_sum.reshape(initial)


def per_component(lookup, freq_index):
    matches = freq_index[:, None] == lax.iota(jnp.int32, lookup.shape[0])[None, :]
    return jnp.sum(jnp.where(matches, lookup[None, :], 0.0), axis=1)


def propagate(energy, ext_mask, courant_y, courant_x):
    for substep in range(SUBSTEPS):
        energy = quickest(energy, courant_y, 1)
        ext_mask = cut_slab(ext_mask, 2, ext_mask.shape[0] - 4, 0)
        energy = quickest(pad_along(energy), courant_x, 2) * ext_mask
    return energy


def on_device(spectrum, transparency, sea_order, speeds, sprinkle, coupling, quad_offsets):
    local_comps = spectrum.shape[0]
    band_rows = spectrum.shape[1]
    first_comp = lax.axis_index("spec") * local_comps
    comp_index = first_comp + lax.iota(jnp.int32, local_comps)
    freq_index = comp_index // NDIR
    dir_index = comp_index % NDIR
    angles = 2.0 * math.pi * (dir_index.astype(jnp.float32) + 0.5) / NDIR
    sines = jnp.sin(angles)
    cosines = jnp.cos(angles)
    speed_comp = per_component(speeds, freq_index)
    spread = per_component(sprinkle, freq_index)
    courant_y = (speed_comp * sines)[:, None, None]
    courant_x = (speed_comp * cosines)[:, None, None]
    spread_y = (spread * (sines * sines + 0.25 * cosines * cosines))[:, None, None]
    spread_x = (spread * (cosines * cosines + 0.25 * sines * sines))[:, None, None]
    stacked = jnp.concatenate([transparency[None], spectrum], axis=0)
    reach = 2 * SUBSTEPS
    extended = extended_2(stacked, (("lat", 1),), reach + 2)
    with_rim = propagate(extended[1:], extended[0], courant_y, courant_x)
    centre = cut_slab(with_rim, 2, band_rows, 1)
    smoothed = (
        centre + spread_y * laplace(with_rim, 1) + spread_x * laplace(pad_along(centre), 2)
    ) * transparency
    flat_cells = smoothed.reshape(local_comps, -1)
    spec_size = lax.axis_size("spec")
    per_dest = SEA_MAX // spec_size
    chunks = CHUNKS if per_dest % CHUNKS == 0 else 1
    sea_cells = sea_order.reshape(-1)[:SEA_MAX].reshape(spec_size, chunks, per_dest // chunks)
    new_cells = flat_cells
    sources = []
    for chunk in range(chunks):
        cells = sea_cells[:, chunk, :].reshape(-1)
        columns = jnp.take(flat_cells, cells, axis=1)
        gathered = lax.all_to_all(columns, "spec", split_axis=1, concat_axis=0, tiled=True)
        source_terms = interact(gathered, coupling, quad_offsets)
        sources.append(source_terms.astype(jnp.bfloat16))
        returned = lax.all_to_all(source_terms, "spec", split_axis=0, concat_axis=1, tiled=True)
        new_cells = new_cells.at[:, cells].add(returned)
    updated = new_cells.reshape(smoothed.shape)
    return (updated, jnp.concatenate(sources, axis=1)[None])


def solution(mesh):
    in_specs = (
        P("spec", "lat", "groups"),
        P("lat", "groups"),
        P("lat", "groups"),
        P(),
        P(),
        P(),
        P(),
    )
    out_specs = (P("spec", "lat", "groups"), P(("groups", "lat"), None, "spec"))
    return jax.shard_map(
        on_device, mesh=mesh, in_specs=in_specs, out_specs=out_specs, check_vma=False
    )
```

```python
import math

import jax
import jax.numpy as jnp
from jax import lax
from jax.sharding import PartitionSpec as P

NDIR = 36
NFREQ = 32
SUBSTEPS = 2
SEA_MAX = 3072


gain_up = 1.25 ** (-4)
gain_down = 0.75 ** (-4)
gain_cross = 0.9375 ** (-4)


def extended_2(block, sides, width):
    for axis, dim in sides:
        count = lax.axis_size(axis)
        forward = [(i, i + 1) for i in range(count - 1)]
        backward = [(target, source) for source, target in forward]
        low = lax.ppermute(
            lax.slice_in_dim(block, block.shape[dim] - width, None, axis=dim), axis, forward
        )
        high = lax.ppermute(lax.slice_in_dim(block, 0, width, axis=dim), axis, backward)
        block = jnp.concatenate([low, block, high], axis=dim)
    return block


def cut_slab(values, offset, length, along):
    return lax.slice_in_dim(values, offset, offset + length, axis=along)


def pad_along(values):
    return jnp.pad(values, ((0, 0), (0, 0), (2, 2)))


def quickest(padded, courant, along):
    length = padded.shape[along] - 4
    before_cell = cut_slab(padded, 0, length + 1, along)
    left_cell = cut_slab(padded, 1, length + 1, along)
    right_cell = cut_slab(padded, 2, length + 1, along)
    after_cell = cut_slab(padded, 3, length + 1, along)
    curvature = jnp.where(
        courant > 0,
        right_cell - 2.0 * left_cell + before_cell,
        after_cell - 2.0 * right_cell + left_cell,
    )
    face_value = (
        0.5 * (left_cell + right_cell)
        - 0.5 * courant * (right_cell - left_cell)
        - (1.0 - courant * courant) / 6.0 * curvature
    )
    face_flux = courant * face_value
    return cut_slab(padded, 2, length, along) - (
        cut_slab(face_flux, 1, length, along) - cut_slab(face_flux, 0, length, along)
    )


def laplace(padded, along):
    length = padded.shape[along] - 4
    centre = cut_slab(padded, 2, length, along)
    near_sum = (
        cut_slab(padded, 1, length, along) + cut_slab(padded, 3, length, along) - 2.0 * centre
    )
    far_sum = cut_slab(padded, 0, length, along) + cut_slab(padded, 4, length, along) - 2.0 * centre
    return 4.0 / 3.0 * near_sum - 1.0 / 12.0 * far_sum


def interact(columns, coupling, quad_offsets):
    initial = columns.shape
    spectra = columns.reshape(NFREQ, NDIR, -1)
    up_freq = quad_offsets[0]
    down_freq = quad_offsets[1]
    dir_one = quad_offsets[2]
    dir_two = quad_offsets[3]
    freq_index = lax.iota(jnp.int32, NFREQ)[:, None, None]
    inside = ((freq_index + up_freq < NFREQ) & (freq_index - down_freq >= 0)).astype(jnp.float32)
    weight = coupling[:, None, None] * inside
    source_sum = jnp.zeros_like(spectra)
    for mirror in (1, -1):
        upper_bin = jnp.roll(jnp.roll(spectra, -up_freq, 0), -mirror * dir_one, 1)
        lower_bin = jnp.roll(jnp.roll(spectra, down_freq, 0), mirror * dir_two, 1)
        squared = spectra * spectra
        transfer = weight * (
            squared * (upper_bin * gain_up + lower_bin * gain_down)
            - 2.0 * gain_cross * spectra * upper_bin * lower_bin
        )
        source_sum = source_sum - 2.0 * transfer
        source_sum = source_sum + jnp.roll(jnp.roll(transfer, up_freq, 0), mirror * dir_one, 1)
        source_sum = source_sum + jnp.roll(jnp.roll(transfer, -down_freq, 0), -mirror * dir_two, 1)
    return source_sum.reshape(initial)


def per_component(lookup, freq_index):
    matches = freq_index[:, None] == lax.iota(jnp.int32, lookup.shape[0])[None, :]
    return jnp.sum(jnp.where(matches, lookup[None, :], 0.0), axis=1)


def propagate(energy, ext_mask, courant_y, courant_x):
    for substep in range(SUBSTEPS):
        energy = quickest(energy, courant_y, 1)
        ext_mask = cut_slab(ext_mask, 2, ext_mask.shape[0] - 4, 0)
        energy = quickest(pad_along(energy), courant_x, 2) * ext_mask
    return energy


def on_device(spectrum, transparency, sea_order, speeds, sprinkle, coupling, quad_offsets):
    local_comps = spectrum.shape[0]
    band_rows = spectrum.shape[1]
    first_comp = lax.axis_index("spec") * local_comps
    comp_index = first_comp + lax.iota(jnp.int32, local_comps)
    freq_index = comp_index // NDIR
    dir_index = comp_index % NDIR
    angles = 2.0 * math.pi * (dir_index.astype(jnp.float32) + 0.5) / NDIR
    sines = jnp.sin(angles)
    cosines = jnp.cos(angles)
    speed_comp = per_component(speeds, freq_index)
    spread = per_component(sprinkle, freq_index)
    courant_y = (speed_comp * sines)[:, None, None]
    courant_x = (speed_comp * cosines)[:, None, None]
    spread_y = (spread * (sines * sines + 0.25 * cosines * cosines))[:, None, None]
    spread_x = (spread * (cosines * cosines + 0.25 * sines * sines))[:, None, None]
    stacked = jnp.concatenate([transparency[None], spectrum], axis=0)
    reach = 2 * SUBSTEPS
    extended = extended_2(stacked, (("lat", 1),), reach + 2)
    with_rim = propagate(extended[1:], extended[0], courant_y, courant_x)
    centre = cut_slab(with_rim, 2, band_rows, 1)
    smoothed = (
        centre + spread_y * laplace(with_rim, 1) + spread_x * laplace(pad_along(centre), 2)
    ) * transparency
    flat_cells = smoothed.reshape(local_comps, -1)
    sea_cells = sea_order.reshape(-1)[:SEA_MAX]
    columns = jnp.take(flat_cells, sea_cells, axis=1)
    gathered = lax.all_to_all(columns, "spec", split_axis=1, concat_axis=0, tiled=True)
    source_terms = interact(gathered, coupling, quad_offsets)
    returned = lax.all_to_all(source_terms.T, "spec", split_axis=1, concat_axis=0, tiled=True)
    placed = jnp.zeros((flat_cells.shape[1], local_comps), jnp.float32).at[sea_cells].set(returned)
    updated = (flat_cells + placed.T).reshape(smoothed.shape)
    return (updated, source_terms.astype(jnp.bfloat16)[None])


def solution(mesh):
    in_specs = (
        P("spec", "lat", "groups"),
        P("lat", "groups"),
        P("lat", "groups"),
        P(),
        P(),
        P(),
        P(),
    )
    out_specs = (P("spec", "lat", "groups"), P(("groups", "lat"), None, "spec"))
    return jax.shard_map(
        on_device, mesh=mesh, in_specs=in_specs, out_specs=out_specs, check_vma=False
    )
```

```python
import math

import jax
import jax.numpy as jnp
from jax import lax
from jax.experimental import pallas as pl
from jax.experimental.pallas import tpu as pltpu
from jax.sharding import PartitionSpec as P

NDIR = 36
NFREQ = 32
SUBSTEPS = 2
SEA_MAX = 3072


gain_up = 1.25 ** (-4)
gain_down = 0.75 ** (-4)
gain_cross = 0.9375 ** (-4)


def extended_2(block, sides, width):
    for axis, dim in sides:
        count = lax.axis_size(axis)
        forward = [(i, i + 1) for i in range(count - 1)]
        backward = [(target, source) for source, target in forward]
        low = lax.ppermute(
            lax.slice_in_dim(block, block.shape[dim] - width, None, axis=dim), axis, forward
        )
        high = lax.ppermute(lax.slice_in_dim(block, 0, width, axis=dim), axis, backward)
        block = jnp.concatenate([low, block, high], axis=dim)
    return block


def cut_slab(values, offset, length, along):
    return lax.slice_in_dim(values, offset, offset + length, axis=along)


def pad_along(values):
    return jnp.pad(values, ((0, 0), (0, 0), (2, 2)))


def quickest(padded, courant, along):
    length = padded.shape[along] - 4
    before_cell = cut_slab(padded, 0, length + 1, along)
    left_cell = cut_slab(padded, 1, length + 1, along)
    right_cell = cut_slab(padded, 2, length + 1, along)
    after_cell = cut_slab(padded, 3, length + 1, along)
    curvature = jnp.where(
        courant > 0,
        right_cell - 2.0 * left_cell + before_cell,
        after_cell - 2.0 * right_cell + left_cell,
    )
    face_value = (
        0.5 * (left_cell + right_cell)
        - 0.5 * courant * (right_cell - left_cell)
        - (1.0 - courant * courant) / 6.0 * curvature
    )
    face_flux = courant * face_value
    return cut_slab(padded, 2, length, along) - (
        cut_slab(face_flux, 1, length, along) - cut_slab(face_flux, 0, length, along)
    )


def laplace(padded, along):
    length = padded.shape[along] - 4
    centre = cut_slab(padded, 2, length, along)
    near_sum = (
        cut_slab(padded, 1, length, along) + cut_slab(padded, 3, length, along) - 2.0 * centre
    )
    far_sum = cut_slab(padded, 0, length, along) + cut_slab(padded, 4, length, along) - 2.0 * centre
    return 4.0 / 3.0 * near_sum - 1.0 / 12.0 * far_sum


def interact_kernel(off_ref, w_ref, e_ref, s_ref, t_ref):
    up_freq = off_ref[0]
    down_freq = off_ref[1]
    dir_one = off_ref[2]
    dir_two = off_ref[3]
    weight = w_ref[...]
    up_shift = (NFREQ - up_freq) % NFREQ
    down_shift = down_freq % NFREQ

    def transfers(d, carry):
        spectra = e_ref[d]
        squared = spectra * spectra
        for slot, mirror in enumerate((1, -1)):
            upper_bin = pltpu.roll(e_ref[(d + mirror * dir_one) % NDIR], up_shift, 0)
            lower_bin = pltpu.roll(e_ref[(d - mirror * dir_two) % NDIR], down_shift, 0)
            t_ref[slot, d] = weight * (
                squared * (upper_bin * gain_up + lower_bin * gain_down)
                - 2.0 * gain_cross * spectra * upper_bin * lower_bin
            )
        return carry

    lax.fori_loop(0, NDIR, transfers, 0)

    def sources(d, carry):
        total = -2.0 * t_ref[0, d] - 2.0 * t_ref[1, d]
        for slot, mirror in enumerate((1, -1)):
            total = total + pltpu.roll(t_ref[slot, (d - mirror * dir_one) % NDIR], up_freq % NFREQ, 0)
            total = total + pltpu.roll(
                t_ref[slot, (d + mirror * dir_two) % NDIR], (NFREQ - down_freq) % NFREQ, 0
            )
        s_ref[d] = total
        return carry

    lax.fori_loop(0, NDIR, sources, 0)


def interact_pallas(columns, coupling, quad_offsets):
    comps, points = columns.shape
    spectra = columns.reshape(NFREQ, NDIR, points).transpose(1, 0, 2)
    freq_index = lax.iota(jnp.int32, NFREQ)
    inside = ((freq_index + quad_offsets[0] < NFREQ) & (freq_index - quad_offsets[1] >= 0)).astype(jnp.float32)
    weight = (coupling * inside)[:, None]
    out = pl.pallas_call(
        interact_kernel,
        out_shape=jax.ShapeDtypeStruct((NDIR, NFREQ, points), jnp.float32),
        in_specs=[
            pl.BlockSpec(memory_space=pltpu.SMEM),
            pl.BlockSpec(memory_space=pltpu.VMEM),
            pl.BlockSpec(memory_space=pltpu.VMEM),
        ],
        out_specs=pl.BlockSpec(memory_space=pltpu.VMEM),
        scratch_shapes=[pltpu.VMEM((2, NDIR, NFREQ, points), jnp.float32)],
    )(quad_offsets, weight, spectra)
    return out.transpose(1, 0, 2).reshape(comps, points)


def per_component(lookup, freq_index):
    matches = freq_index[:, None] == lax.iota(jnp.int32, lookup.shape[0])[None, :]
    return jnp.sum(jnp.where(matches, lookup[None, :], 0.0), axis=1)


def propagate(energy, ext_mask, courant_y, courant_x):
    for substep in range(SUBSTEPS):
        energy = quickest(energy, courant_y, 1)
        ext_mask = cut_slab(ext_mask, 2, ext_mask.shape[0] - 4, 0)
        energy = quickest(pad_along(energy), courant_x, 2) * ext_mask
    return energy


def on_device(spectrum, transparency, sea_order, speeds, sprinkle, coupling, quad_offsets):
    local_comps = spectrum.shape[0]
    band_rows = spectrum.shape[1]
    first_comp = lax.axis_index("spec") * local_comps
    comp_index = first_comp + lax.iota(jnp.int32, local_comps)
    freq_index = comp_index // NDIR
    dir_index = comp_index % NDIR
    angles = 2.0 * math.pi * (dir_index.astype(jnp.float32) + 0.5) / NDIR
    sines = jnp.sin(angles)
    cosines = jnp.cos(angles)
    speed_comp = per_component(speeds, freq_index)
    spread = per_component(sprinkle, freq_index)
    courant_y = (speed_comp * sines)[:, None, None]
    courant_x = (speed_comp * cosines)[:, None, None]
    spread_y = (spread * (sines * sines + 0.25 * cosines * cosines))[:, None, None]
    spread_x = (spread * (cosines * cosines + 0.25 * sines * sines))[:, None, None]
    stacked = jnp.concatenate([transparency[None], spectrum], axis=0)
    reach = 2 * SUBSTEPS
    extended = extended_2(stacked, (("lat", 1),), reach + 2)
    with_rim = propagate(extended[1:], extended[0], courant_y, courant_x)
    centre = cut_slab(with_rim, 2, band_rows, 1)
    smoothed = (
        centre + spread_y * laplace(with_rim, 1) + spread_x * laplace(pad_along(centre), 2)
    ) * transparency
    flat_cells = smoothed.reshape(local_comps, -1)
    sea_cells = sea_order.reshape(-1)[:SEA_MAX]
    columns = jnp.take(flat_cells, sea_cells, axis=1)
    gathered = lax.all_to_all(columns, "spec", split_axis=1, concat_axis=0, tiled=True)
    source_terms = interact_pallas(gathered, coupling, quad_offsets)
    returned = lax.all_to_all(source_terms, "spec", split_axis=0, concat_axis=1, tiled=True)
    new_cells = flat_cells.at[:, sea_cells].add(returned)
    updated = new_cells.reshape(smoothed.shape)
    return (updated, source_terms.astype(jnp.bfloat16)[None])


def solution(mesh):
    in_specs = (
        P("spec", "lat", "groups"),
        P("lat", "groups"),
        P("lat", "groups"),
        P(),
        P(),
        P(),
        P(),
    )
    out_specs = (P("spec", "lat", "groups"), P(("groups", "lat"), None, "spec"))
    return jax.shard_map(
        on_device, mesh=mesh, in_specs=in_specs, out_specs=out_specs, check_vma=False
    )
```

```python
import math

import jax
import jax.numpy as jnp
from jax import lax
from jax.experimental import pallas as pl
from jax.experimental.pallas import tpu as pltpu
from jax.sharding import PartitionSpec as P

NDIR = 36
NFREQ = 32
SUBSTEPS = 2
SEA_MAX = 3072


gain_up = 1.25 ** (-4)
gain_down = 0.75 ** (-4)
gain_cross = 0.9375 ** (-4)


def extended_2(block, sides, width):
    for axis, dim in sides:
        count = lax.axis_size(axis)
        forward = [(i, i + 1) for i in range(count - 1)]
        backward = [(target, source) for source, target in forward]
        low = lax.ppermute(
            lax.slice_in_dim(block, block.shape[dim] - width, None, axis=dim), axis, forward
        )
        high = lax.ppermute(lax.slice_in_dim(block, 0, width, axis=dim), axis, backward)
        block = jnp.concatenate([low, block, high], axis=dim)
    return block


def cut_slab(values, offset, length, along):
    return lax.slice_in_dim(values, offset, offset + length, axis=along)


def pad_along(values):
    return jnp.pad(values, ((0, 0), (0, 0), (2, 2)))


def quickest(padded, courant, along):
    length = padded.shape[along] - 4
    before_cell = cut_slab(padded, 0, length + 1, along)
    left_cell = cut_slab(padded, 1, length + 1, along)
    right_cell = cut_slab(padded, 2, length + 1, along)
    after_cell = cut_slab(padded, 3, length + 1, along)
    curvature = jnp.where(
        courant > 0,
        right_cell - 2.0 * left_cell + before_cell,
        after_cell - 2.0 * right_cell + left_cell,
    )
    face_value = (
        0.5 * (left_cell + right_cell)
        - 0.5 * courant * (right_cell - left_cell)
        - (1.0 - courant * courant) / 6.0 * curvature
    )
    face_flux = courant * face_value
    return cut_slab(padded, 2, length, along) - (
        cut_slab(face_flux, 1, length, along) - cut_slab(face_flux, 0, length, along)
    )


def laplace(padded, along):
    length = padded.shape[along] - 4
    centre = cut_slab(padded, 2, length, along)
    near_sum = (
        cut_slab(padded, 1, length, along) + cut_slab(padded, 3, length, along) - 2.0 * centre
    )
    far_sum = cut_slab(padded, 0, length, along) + cut_slab(padded, 4, length, along) - 2.0 * centre
    return 4.0 / 3.0 * near_sum - 1.0 / 12.0 * far_sum


def interact_kernel(off_ref, w_ref, e_ref, s_ref, t_ref):
    up_freq = off_ref[0]
    down_freq = off_ref[1]
    dir_one = off_ref[2]
    dir_two = off_ref[3]
    weight = w_ref[...]
    up_shift = (NFREQ - up_freq) % NFREQ
    down_shift = down_freq % NFREQ

    def transfers(d, carry):
        spectra = e_ref[d]
        squared = spectra * spectra
        for slot, mirror in enumerate((1, -1)):
            upper_bin = pltpu.roll(e_ref[(d + mirror * dir_one) % NDIR], up_shift, 0)
            lower_bin = pltpu.roll(e_ref[(d - mirror * dir_two) % NDIR], down_shift, 0)
            t_ref[slot, d] = weight * (
                squared * (upper_bin * gain_up + lower_bin * gain_down)
                - 2.0 * gain_cross * spectra * upper_bin * lower_bin
            )
        return carry

    lax.fori_loop(0, NDIR, transfers, 0)

    def sources(d, carry):
        total = -2.0 * t_ref[0, d] - 2.0 * t_ref[1, d]
        for slot, mirror in enumerate((1, -1)):
            total = total + pltpu.roll(t_ref[slot, (d - mirror * dir_one) % NDIR], up_freq % NFREQ, 0)
            total = total + pltpu.roll(
                t_ref[slot, (d + mirror * dir_two) % NDIR], (NFREQ - down_freq) % NFREQ, 0
            )
        s_ref[d] = total
        return carry

    lax.fori_loop(0, NDIR, sources, 0)


def interact_pallas(columns, coupling, quad_offsets):
    comps, points = columns.shape
    spectra = columns.reshape(NFREQ, NDIR, points).transpose(1, 0, 2)
    freq_index = lax.iota(jnp.int32, NFREQ)
    inside = ((freq_index + quad_offsets[0] < NFREQ) & (freq_index - quad_offsets[1] >= 0)).astype(jnp.float32)
    weight = (coupling * inside)[:, None]
    out = pl.pallas_call(
        interact_kernel,
        out_shape=jax.ShapeDtypeStruct((NDIR, NFREQ, points), jnp.float32),
        in_specs=[
            pl.BlockSpec(memory_space=pltpu.SMEM),
            pl.BlockSpec(memory_space=pltpu.VMEM),
            pl.BlockSpec(memory_space=pltpu.VMEM),
        ],
        out_specs=pl.BlockSpec(memory_space=pltpu.VMEM),
        scratch_shapes=[pltpu.VMEM((2, NDIR, NFREQ, points), jnp.float32)],
    )(quad_offsets, weight, spectra)
    return out.transpose(1, 0, 2).reshape(comps, points)


def per_component(lookup, freq_index):
    matches = freq_index[:, None] == lax.iota(jnp.int32, lookup.shape[0])[None, :]
    return jnp.sum(jnp.where(matches, lookup[None, :], 0.0), axis=1)


def propagate(energy, ext_mask, courant_y, courant_x):
    for substep in range(SUBSTEPS):
        energy = quickest(energy, courant_y, 1)
        ext_mask = cut_slab(ext_mask, 2, ext_mask.shape[0] - 4, 0)
        energy = quickest(pad_along(energy), courant_x, 2) * ext_mask
    return energy


def on_device(spectrum, transparency, sea_order, speeds, sprinkle, coupling, quad_offsets):
    local_comps = spectrum.shape[0]
    band_rows = spectrum.shape[1]
    first_comp = lax.axis_index("spec") * local_comps
    comp_index = first_comp + lax.iota(jnp.int32, local_comps)
    freq_index = comp_index // NDIR
    dir_index = comp_index % NDIR
    angles = 2.0 * math.pi * (dir_index.astype(jnp.float32) + 0.5) / NDIR
    sines = jnp.sin(angles)
    cosines = jnp.cos(angles)
    speed_comp = per_component(speeds, freq_index)
    spread = per_component(sprinkle, freq_index)
    courant_y = (speed_comp * sines)[:, None, None]
    courant_x = (speed_comp * cosines)[:, None, None]
    spread_y = (spread * (sines * sines + 0.25 * cosines * cosines))[:, None, None]
    spread_x = (spread * (cosines * cosines + 0.25 * sines * sines))[:, None, None]
    stacked = jnp.concatenate([transparency[None], spectrum], axis=0)
    reach = 2 * SUBSTEPS
    extended = extended_2(stacked, (("lat", 1),), reach + 2)
    with_rim = propagate(extended[1:], extended[0], courant_y, courant_x)
    centre = cut_slab(with_rim, 2, band_rows, 1)
    smoothed = (
        centre + spread_y * laplace(with_rim, 1) + spread_x * laplace(pad_along(centre), 2)
    ) * transparency
    flat_cells = smoothed.reshape(local_comps, -1)
    sea_cells = sea_order.reshape(-1)[:SEA_MAX]
    columns = flat_cells.at[:, sea_cells].get(mode="promise_in_bounds", unique_indices=True)
    gathered = lax.all_to_all(columns, "spec", split_axis=1, concat_axis=0, tiled=True)
    source_terms = interact_pallas(gathered, coupling, quad_offsets)
    returned = lax.all_to_all(source_terms, "spec", split_axis=0, concat_axis=1, tiled=True)
    new_cells = flat_cells.at[:, sea_cells].add(
        returned, mode="promise_in_bounds", unique_indices=True
    )
    updated = new_cells.reshape(smoothed.shape)
    return (updated, source_terms.astype(jnp.bfloat16)[None])


def solution(mesh):
    in_specs = (
        P("spec", "lat", "groups"),
        P("lat", "groups"),
        P("lat", "groups"),
        P(),
        P(),
        P(),
        P(),
    )
    out_specs = (P("spec", "lat", "groups"), P(("groups", "lat"), None, "spec"))
    return jax.shard_map(
        on_device, mesh=mesh, in_specs=in_specs, out_specs=out_specs, check_vma=False
    )
```

```python
import math

import jax
import jax.numpy as jnp
from jax import lax
from jax.experimental import pallas as pl
from jax.experimental.pallas import tpu as pltpu
from jax.sharding import PartitionSpec as P

NDIR = 36
NFREQ = 32
SUBSTEPS = 2
SEA_MAX = 3072


gain_up = 1.25 ** (-4)
gain_down = 0.75 ** (-4)
gain_cross = 0.9375 ** (-4)


def extended_2(block, sides, width):
    for axis, dim in sides:
        count = lax.axis_size(axis)
        forward = [(i, i + 1) for i in range(count - 1)]
        backward = [(target, source) for source, target in forward]
        low = lax.ppermute(
            lax.slice_in_dim(block, block.shape[dim] - width, None, axis=dim), axis, forward
        )
        high = lax.ppermute(lax.slice_in_dim(block, 0, width, axis=dim), axis, backward)
        block = jnp.concatenate([low, block, high], axis=dim)
    return block


def cut_slab(values, offset, length, along):
    return lax.slice_in_dim(values, offset, offset + length, axis=along)


def pad_along(values):
    return jnp.pad(values, ((0, 0), (0, 0), (2, 2)))


def quickest(padded, courant, along):
    length = padded.shape[along] - 4
    before_cell = cut_slab(padded, 0, length + 1, along)
    left_cell = cut_slab(padded, 1, length + 1, along)
    right_cell = cut_slab(padded, 2, length + 1, along)
    after_cell = cut_slab(padded, 3, length + 1, along)
    curvature = jnp.where(
        courant > 0,
        right_cell - 2.0 * left_cell + before_cell,
        after_cell - 2.0 * right_cell + left_cell,
    )
    face_value = (
        0.5 * (left_cell + right_cell)
        - 0.5 * courant * (right_cell - left_cell)
        - (1.0 - courant * courant) / 6.0 * curvature
    )
    face_flux = courant * face_value
    return cut_slab(padded, 2, length, along) - (
        cut_slab(face_flux, 1, length, along) - cut_slab(face_flux, 0, length, along)
    )


def laplace(padded, along):
    length = padded.shape[along] - 4
    centre = cut_slab(padded, 2, length, along)
    near_sum = (
        cut_slab(padded, 1, length, along) + cut_slab(padded, 3, length, along) - 2.0 * centre
    )
    far_sum = cut_slab(padded, 0, length, along) + cut_slab(padded, 4, length, along) - 2.0 * centre
    return 4.0 / 3.0 * near_sum - 1.0 / 12.0 * far_sum


def interact_kernel(off_ref, w_ref, e_ref, s_ref, t_ref):
    up_freq = off_ref[0]
    down_freq = off_ref[1]
    dir_one = off_ref[2]
    dir_two = off_ref[3]
    weight = w_ref[...]
    up_shift = (NFREQ - up_freq) % NFREQ
    down_shift = down_freq % NFREQ

    def transfers(d, carry):
        spectra = e_ref[d]
        squared = spectra * spectra
        for slot, mirror in enumerate((1, -1)):
            upper_bin = pltpu.roll(e_ref[(d + mirror * dir_one) % NDIR], up_shift, 0)
            lower_bin = pltpu.roll(e_ref[(d - mirror * dir_two) % NDIR], down_shift, 0)
            t_ref[slot, d] = weight * (
                squared * (upper_bin * gain_up + lower_bin * gain_down)
                - 2.0 * gain_cross * spectra * upper_bin * lower_bin
            )
        return carry

    lax.fori_loop(0, NDIR, transfers, 0)

    def sources(d, carry):
        total = -2.0 * t_ref[0, d] - 2.0 * t_ref[1, d]
        for slot, mirror in enumerate((1, -1)):
            total = total + pltpu.roll(t_ref[slot, (d - mirror * dir_one) % NDIR], up_freq % NFREQ, 0)
            total = total + pltpu.roll(
                t_ref[slot, (d + mirror * dir_two) % NDIR], (NFREQ - down_freq) % NFREQ, 0
            )
        s_ref[d] = total
        return carry

    lax.fori_loop(0, NDIR, sources, 0)


def interact_pallas(columns, coupling, quad_offsets):
    comps, points = columns.shape
    spectra = columns.reshape(NFREQ, NDIR, points).transpose(1, 0, 2)
    freq_index = lax.iota(jnp.int32, NFREQ)
    inside = ((freq_index + quad_offsets[0] < NFREQ) & (freq_index - quad_offsets[1] >= 0)).astype(jnp.float32)
    weight = (coupling * inside)[:, None]
    out = pl.pallas_call(
        interact_kernel,
        out_shape=jax.ShapeDtypeStruct((NDIR, NFREQ, points), jnp.float32),
        in_specs=[
            pl.BlockSpec(memory_space=pltpu.SMEM),
            pl.BlockSpec(memory_space=pltpu.VMEM),
            pl.BlockSpec(memory_space=pltpu.VMEM),
        ],
        out_specs=pl.BlockSpec(memory_space=pltpu.VMEM),
        scratch_shapes=[pltpu.VMEM((2, NDIR, NFREQ, points), jnp.float32)],
    )(quad_offsets, weight, spectra)
    return out.transpose(1, 0, 2).reshape(comps, points)


def per_component(lookup, freq_index):
    matches = freq_index[:, None] == lax.iota(jnp.int32, lookup.shape[0])[None, :]
    return jnp.sum(jnp.where(matches, lookup[None, :], 0.0), axis=1)


def propagate(energy, ext_mask, courant_y, courant_x):
    for substep in range(SUBSTEPS):
        energy = quickest(energy, courant_y, 1)
        ext_mask = cut_slab(ext_mask, 2, ext_mask.shape[0] - 4, 0)
        energy = quickest(pad_along(energy), courant_x, 2) * ext_mask
    return energy


def on_device(spectrum, transparency, sea_order, speeds, sprinkle, coupling, quad_offsets):
    local_comps = spectrum.shape[0]
    band_rows = spectrum.shape[1]
    first_comp = lax.axis_index("spec") * local_comps
    comp_index = first_comp + lax.iota(jnp.int32, local_comps)
    freq_index = comp_index // NDIR
    dir_index = comp_index % NDIR
    angles = 2.0 * math.pi * (dir_index.astype(jnp.float32) + 0.5) / NDIR
    sines = jnp.sin(angles)
    cosines = jnp.cos(angles)
    speed_comp = per_component(speeds, freq_index)
    spread = per_component(sprinkle, freq_index)
    courant_y = (speed_comp * sines)[:, None, None]
    courant_x = (speed_comp * cosines)[:, None, None]
    spread_y = (spread * (sines * sines + 0.25 * cosines * cosines))[:, None, None]
    spread_x = (spread * (cosines * cosines + 0.25 * sines * sines))[:, None, None]
    stacked = jnp.concatenate([transparency[None], spectrum], axis=0)
    reach = 2 * SUBSTEPS
    extended = extended_2(stacked, (("lat", 1),), reach + 2)
    with_rim = propagate(extended[1:], extended[0], courant_y, courant_x)
    centre = cut_slab(with_rim, 2, band_rows, 1)
    smoothed = (
        centre + spread_y * laplace(with_rim, 1) + spread_x * laplace(pad_along(centre), 2)
    ) * transparency
    flat_cells = smoothed.reshape(local_comps, -1)
    spec_size = lax.axis_size("spec")
    me = lax.axis_index("spec")
    per_dest = SEA_MAX // spec_size
    cells = sea_order.reshape(-1)[:SEA_MAX].reshape(spec_size, per_dest)
    pieces = []
    for shift in range(spec_size):
        dest = (me + shift) % spec_size
        block_cells = lax.dynamic_index_in_dim(cells, dest, 0, keepdims=False)
        block = flat_cells.at[:, block_cells].get(mode="promise_in_bounds", unique_indices=True)
        if shift:
            pairs = [(s, (s + shift) % spec_size) for s in range(spec_size)]
            block = lax.ppermute(block, "spec", pairs)
        pieces.append(block)
    by_shift = jnp.stack(pieces[:1] + pieces[:0:-1])
    gathered = jnp.roll(by_shift, me, axis=0).reshape(-1, per_dest)
    source_terms = interact_pallas(gathered, coupling, quad_offsets)
    new_cells = flat_cells
    for shift in range(spec_size):
        dest = (me + shift) % spec_size
        src = (me - shift) % spec_size
        block = lax.dynamic_slice_in_dim(source_terms, dest * local_comps, local_comps, 0)
        if shift:
            pairs = [(s, (s + shift) % spec_size) for s in range(spec_size)]
            block = lax.ppermute(block, "spec", pairs)
        block_cells = lax.dynamic_index_in_dim(cells, src, 0, keepdims=False)
        new_cells = new_cells.at[:, block_cells].add(
            block, mode="promise_in_bounds", unique_indices=True
        )
    updated = new_cells.reshape(smoothed.shape)
    return (updated, source_terms.astype(jnp.bfloat16)[None])


def solution(mesh):
    in_specs = (
        P("spec", "lat", "groups"),
        P("lat", "groups"),
        P("lat", "groups"),
        P(),
        P(),
        P(),
        P(),
    )
    out_specs = (P("spec", "lat", "groups"), P(("groups", "lat"), None, "spec"))
    return jax.shard_map(
        on_device, mesh=mesh, in_specs=in_specs, out_specs=out_specs, check_vma=False
    )
```

```python
import math

import jax
import jax.numpy as jnp
from jax import lax
from jax.experimental import pallas as pl
from jax.experimental.pallas import tpu as pltpu
from jax.sharding import PartitionSpec as P

NDIR = 36
NFREQ = 32
SUBSTEPS = 2
SEA_MAX = 3072


gain_up = 1.25 ** (-4)
gain_down = 0.75 ** (-4)
gain_cross = 0.9375 ** (-4)


def extended_2(block, sides, width):
    for axis, dim in sides:
        count = lax.axis_size(axis)
        forward = [(i, i + 1) for i in range(count - 1)]
        backward = [(target, source) for source, target in forward]
        low = lax.ppermute(
            lax.slice_in_dim(block, block.shape[dim] - width, None, axis=dim), axis, forward
        )
        high = lax.ppermute(lax.slice_in_dim(block, 0, width, axis=dim), axis, backward)
        block = jnp.concatenate([low, block, high], axis=dim)
    return block


def cut_slab(values, offset, length, along):
    return lax.slice_in_dim(values, offset, offset + length, axis=along)


def pad_along(values):
    return jnp.pad(values, ((0, 0), (0, 0), (2, 2)))


def quickest(padded, courant, along):
    length = padded.shape[along] - 4
    before_cell = cut_slab(padded, 0, length + 1, along)
    left_cell = cut_slab(padded, 1, length + 1, along)
    right_cell = cut_slab(padded, 2, length + 1, along)
    after_cell = cut_slab(padded, 3, length + 1, along)
    curvature = jnp.where(
        courant > 0,
        right_cell - 2.0 * left_cell + before_cell,
        after_cell - 2.0 * right_cell + left_cell,
    )
    face_value = (
        0.5 * (left_cell + right_cell)
        - 0.5 * courant * (right_cell - left_cell)
        - (1.0 - courant * courant) / 6.0 * curvature
    )
    face_flux = courant * face_value
    return cut_slab(padded, 2, length, along) - (
        cut_slab(face_flux, 1, length, along) - cut_slab(face_flux, 0, length, along)
    )


def laplace(padded, along):
    length = padded.shape[along] - 4
    centre = cut_slab(padded, 2, length, along)
    near_sum = (
        cut_slab(padded, 1, length, along) + cut_slab(padded, 3, length, along) - 2.0 * centre
    )
    far_sum = cut_slab(padded, 0, length, along) + cut_slab(padded, 4, length, along) - 2.0 * centre
    return 4.0 / 3.0 * near_sum - 1.0 / 12.0 * far_sum


def interact_kernel(off_ref, w_ref, e_ref, s_ref, t_ref):
    up_freq = off_ref[0]
    down_freq = off_ref[1]
    dir_one = off_ref[2]
    dir_two = off_ref[3]
    weight = w_ref[...]
    up_shift = (NFREQ - up_freq) % NFREQ
    down_shift = down_freq % NFREQ

    def transfers(d, carry):
        spectra = e_ref[d]
        squared = spectra * spectra
        for slot, mirror in enumerate((1, -1)):
            upper_bin = pltpu.roll(e_ref[(d + mirror * dir_one) % NDIR], up_shift, 0)
            lower_bin = pltpu.roll(e_ref[(d - mirror * dir_two) % NDIR], down_shift, 0)
            t_ref[slot, d] = weight * (
                squared * (upper_bin * gain_up + lower_bin * gain_down)
                - 2.0 * gain_cross * spectra * upper_bin * lower_bin
            )
        return carry

    lax.fori_loop(0, NDIR, transfers, 0)

    def sources(d, carry):
        total = -2.0 * t_ref[0, d] - 2.0 * t_ref[1, d]
        for slot, mirror in enumerate((1, -1)):
            total = total + pltpu.roll(t_ref[slot, (d - mirror * dir_one) % NDIR], up_freq % NFREQ, 0)
            total = total + pltpu.roll(
                t_ref[slot, (d + mirror * dir_two) % NDIR], (NFREQ - down_freq) % NFREQ, 0
            )
        s_ref[d] = total
        return carry

    lax.fori_loop(0, NDIR, sources, 0)


def interact_pallas(columns, coupling, quad_offsets):
    comps, points = columns.shape
    spectra = columns.reshape(NFREQ, NDIR, points).transpose(1, 0, 2)
    freq_index = lax.iota(jnp.int32, NFREQ)
    inside = ((freq_index + quad_offsets[0] < NFREQ) & (freq_index - quad_offsets[1] >= 0)).astype(jnp.float32)
    weight = (coupling * inside)[:, None]
    out = pl.pallas_call(
        interact_kernel,
        out_shape=jax.ShapeDtypeStruct((NDIR, NFREQ, points), jnp.float32),
        in_specs=[
            pl.BlockSpec(memory_space=pltpu.SMEM),
            pl.BlockSpec(memory_space=pltpu.VMEM),
            pl.BlockSpec(memory_space=pltpu.VMEM),
        ],
        out_specs=pl.BlockSpec(memory_space=pltpu.VMEM),
        scratch_shapes=[pltpu.VMEM((2, NDIR, NFREQ, points), jnp.float32)],
    )(quad_offsets, weight, spectra)
    return out.transpose(1, 0, 2).reshape(comps, points)


def per_component(lookup, freq_index):
    matches = freq_index[:, None] == lax.iota(jnp.int32, lookup.shape[0])[None, :]
    return jnp.sum(jnp.where(matches, lookup[None, :], 0.0), axis=1)


def propagate(energy, ext_mask, courant_y, courant_x):
    for substep in range(SUBSTEPS):
        energy = quickest(energy, courant_y, 1)
        ext_mask = cut_slab(ext_mask, 2, ext_mask.shape[0] - 4, 0)
        energy = quickest(pad_along(energy), courant_x, 2) * ext_mask
    return energy


def on_device(spectrum, transparency, sea_order, speeds, sprinkle, coupling, quad_offsets):
    local_comps = spectrum.shape[0]
    band_rows = spectrum.shape[1]
    first_comp = lax.axis_index("spec") * local_comps
    comp_index = first_comp + lax.iota(jnp.int32, local_comps)
    freq_index = comp_index // NDIR
    dir_index = comp_index % NDIR
    angles = 2.0 * math.pi * (dir_index.astype(jnp.float32) + 0.5) / NDIR
    sines = jnp.sin(angles)
    cosines = jnp.cos(angles)
    speed_comp = per_component(speeds, freq_index)
    spread = per_component(sprinkle, freq_index)
    courant_y = (speed_comp * sines)[:, None, None]
    courant_x = (speed_comp * cosines)[:, None, None]
    spread_y = (spread * (sines * sines + 0.25 * cosines * cosines))[:, None, None]
    spread_x = (spread * (cosines * cosines + 0.25 * sines * sines))[:, None, None]
    stacked = jnp.concatenate([transparency[None], spectrum], axis=0)
    reach = 2 * SUBSTEPS
    extended = extended_2(stacked, (("lat", 1),), reach + 2)
    with_rim = propagate(extended[1:], extended[0], courant_y, courant_x)
    centre = cut_slab(with_rim, 2, band_rows, 1)
    smoothed = (
        centre + spread_y * laplace(with_rim, 1) + spread_x * laplace(pad_along(centre), 2)
    ) * transparency
    flat_cells = smoothed.reshape(local_comps, -1)
    spec_size = lax.axis_size("spec")
    me = lax.axis_index("spec")
    per_dest = SEA_MAX // spec_size
    cells = sea_order.reshape(-1)[:SEA_MAX].reshape(spec_size, per_dest)
    send_cells = jnp.roll(cells, -me, axis=0).reshape(-1)
    columns = flat_cells.at[:, send_cells].get(mode="promise_in_bounds", unique_indices=True)
    pieces = []
    for shift in range(spec_size):
        block = lax.slice_in_dim(columns, shift * per_dest, (shift + 1) * per_dest, axis=1)
        if shift:
            pairs = [(s, (s + shift) % spec_size) for s in range(spec_size)]
            block = lax.ppermute(block, "spec", pairs)
        pieces.append(block)
    by_shift = jnp.stack(pieces[:1] + pieces[:0:-1])
    gathered = jnp.roll(by_shift, me, axis=0).reshape(-1, per_dest)
    source_terms = interact_pallas(gathered, coupling, quad_offsets)
    by_dest = jnp.roll(source_terms.reshape(spec_size, local_comps, per_dest), -me, axis=0)
    returned = []
    for shift in range(spec_size):
        block = by_dest[shift]
        if shift:
            pairs = [(s, (s + shift) % spec_size) for s in range(spec_size)]
            block = lax.ppermute(block, "spec", pairs)
        returned.append(block)
    recv_cells = jnp.roll(cells[::-1], me + 1, axis=0).reshape(-1)
    new_cells = flat_cells.at[:, recv_cells].add(
        jnp.concatenate(returned, axis=1), mode="promise_in_bounds", unique_indices=True
    )
    updated = new_cells.reshape(smoothed.shape)
    return (updated, source_terms.astype(jnp.bfloat16)[None])


def solution(mesh):
    in_specs = (
        P("spec", "lat", "groups"),
        P("lat", "groups"),
        P("lat", "groups"),
        P(),
        P(),
        P(),
        P(),
    )
    out_specs = (P("spec", "lat", "groups"), P(("groups", "lat"), None, "spec"))
    return jax.shard_map(
        on_device, mesh=mesh, in_specs=in_specs, out_specs=out_specs, check_vma=False
    )
```

```python
import math

import jax
import jax.numpy as jnp
from jax import lax
from jax.experimental import pallas as pl
from jax.experimental.pallas import tpu as pltpu
from jax.sharding import PartitionSpec as P

NDIR = 36
NFREQ = 32
SUBSTEPS = 2
SEA_MAX = 3072


gain_up = 1.25 ** (-4)
gain_down = 0.75 ** (-4)
gain_cross = 0.9375 ** (-4)


def extended_2(block, sides, width):
    for axis, dim in sides:
        count = lax.axis_size(axis)
        bottom = lax.slice_in_dim(block, block.shape[dim] - width, None, axis=dim)
        top = lax.slice_in_dim(block, 0, width, axis=dim)
        if count == 2:
            first = lax.axis_index(axis) == 0
            swapped = lax.ppermute(jnp.where(first, bottom, top), axis, [(0, 1), (1, 0)])
            low = jnp.where(first, 0.0, swapped)
            high = jnp.where(first, swapped, 0.0)
        else:
            forward = [(i, i + 1) for i in range(count - 1)]
            backward = [(target, source) for source, target in forward]
            low = lax.ppermute(bottom, axis, forward)
            high = lax.ppermute(top, axis, backward)
        block = jnp.concatenate([low, block, high], axis=dim)
    return block


def cut_slab(values, offset, length, along):
    return lax.slice_in_dim(values, offset, offset + length, axis=along)


def pad_along(values):
    return jnp.pad(values, ((0, 0), (0, 0), (2, 2)))


def quickest(padded, courant, along):
    length = padded.shape[along] - 4
    before_cell = cut_slab(padded, 0, length + 1, along)
    left_cell = cut_slab(padded, 1, length + 1, along)
    right_cell = cut_slab(padded, 2, length + 1, along)
    after_cell = cut_slab(padded, 3, length + 1, along)
    curvature = jnp.where(
        courant > 0,
        right_cell - 2.0 * left_cell + before_cell,
        after_cell - 2.0 * right_cell + left_cell,
    )
    face_value = (
        0.5 * (left_cell + right_cell)
        - 0.5 * courant * (right_cell - left_cell)
        - (1.0 - courant * courant) / 6.0 * curvature
    )
    face_flux = courant * face_value
    return cut_slab(padded, 2, length, along) - (
        cut_slab(face_flux, 1, length, along) - cut_slab(face_flux, 0, length, along)
    )


def laplace(padded, along):
    length = padded.shape[along] - 4
    centre = cut_slab(padded, 2, length, along)
    near_sum = (
        cut_slab(padded, 1, length, along) + cut_slab(padded, 3, length, along) - 2.0 * centre
    )
    far_sum = cut_slab(padded, 0, length, along) + cut_slab(padded, 4, length, along) - 2.0 * centre
    return 4.0 / 3.0 * near_sum - 1.0 / 12.0 * far_sum


def interact_kernel(off_ref, w_ref, e_ref, s_ref, t_ref):
    up_freq = off_ref[0]
    down_freq = off_ref[1]
    dir_one = off_ref[2]
    dir_two = off_ref[3]
    weight = w_ref[...]
    up_shift = (NFREQ - up_freq) % NFREQ
    down_shift = down_freq % NFREQ

    def transfers(d, carry):
        spectra = e_ref[d]
        squared = spectra * spectra
        for slot, mirror in enumerate((1, -1)):
            upper_bin = pltpu.roll(e_ref[(d + mirror * dir_one) % NDIR], up_shift, 0)
            lower_bin = pltpu.roll(e_ref[(d - mirror * dir_two) % NDIR], down_shift, 0)
            t_ref[slot, d] = weight * (
                squared * (upper_bin * gain_up + lower_bin * gain_down)
                - 2.0 * gain_cross * spectra * upper_bin * lower_bin
            )
        return carry

    lax.fori_loop(0, NDIR, transfers, 0)

    def sources(d, carry):
        total = -2.0 * t_ref[0, d] - 2.0 * t_ref[1, d]
        for slot, mirror in enumerate((1, -1)):
            total = total + pltpu.roll(t_ref[slot, (d - mirror * dir_one) % NDIR], up_freq % NFREQ, 0)
            total = total + pltpu.roll(
                t_ref[slot, (d + mirror * dir_two) % NDIR], (NFREQ - down_freq) % NFREQ, 0
            )
        s_ref[d] = total
        return carry

    lax.fori_loop(0, NDIR, sources, 0)


def interact_pallas(columns, coupling, quad_offsets):
    comps, points = columns.shape
    spectra = columns.reshape(NFREQ, NDIR, points).transpose(1, 0, 2)
    freq_index = lax.iota(jnp.int32, NFREQ)
    inside = ((freq_index + quad_offsets[0] < NFREQ) & (freq_index - quad_offsets[1] >= 0)).astype(jnp.float32)
    weight = (coupling * inside)[:, None]
    out = pl.pallas_call(
        interact_kernel,
        out_shape=jax.ShapeDtypeStruct((NDIR, NFREQ, points), jnp.float32),
        in_specs=[
            pl.BlockSpec(memory_space=pltpu.SMEM),
            pl.BlockSpec(memory_space=pltpu.VMEM),
            pl.BlockSpec(memory_space=pltpu.VMEM),
        ],
        out_specs=pl.BlockSpec(memory_space=pltpu.VMEM),
        scratch_shapes=[pltpu.VMEM((2, NDIR, NFREQ, points), jnp.float32)],
    )(quad_offsets, weight, spectra)
    return out.transpose(1, 0, 2).reshape(comps, points)


def per_component(lookup, freq_index):
    matches = freq_index[:, None] == lax.iota(jnp.int32, lookup.shape[0])[None, :]
    return jnp.sum(jnp.where(matches, lookup[None, :], 0.0), axis=1)


def propagate(energy, ext_mask, courant_y, courant_x):
    for substep in range(SUBSTEPS):
        energy = quickest(energy, courant_y, 1)
        ext_mask = cut_slab(ext_mask, 2, ext_mask.shape[0] - 4, 0)
        energy = quickest(pad_along(energy), courant_x, 2) * ext_mask
    return energy


def on_device(spectrum, transparency, sea_order, speeds, sprinkle, coupling, quad_offsets):
    local_comps = spectrum.shape[0]
    band_rows = spectrum.shape[1]
    first_comp = lax.axis_index("spec") * local_comps
    comp_index = first_comp + lax.iota(jnp.int32, local_comps)
    freq_index = comp_index // NDIR
    dir_index = comp_index % NDIR
    angles = 2.0 * math.pi * (dir_index.astype(jnp.float32) + 0.5) / NDIR
    sines = jnp.sin(angles)
    cosines = jnp.cos(angles)
    speed_comp = per_component(speeds, freq_index)
    spread = per_component(sprinkle, freq_index)
    courant_y = (speed_comp * sines)[:, None, None]
    courant_x = (speed_comp * cosines)[:, None, None]
    spread_y = (spread * (sines * sines + 0.25 * cosines * cosines))[:, None, None]
    spread_x = (spread * (cosines * cosines + 0.25 * sines * sines))[:, None, None]
    stacked = jnp.concatenate([transparency[None], spectrum], axis=0)
    reach = 2 * SUBSTEPS
    extended = extended_2(stacked, (("lat", 1),), reach + 2)
    with_rim = propagate(extended[1:], extended[0], courant_y, courant_x)
    centre = cut_slab(with_rim, 2, band_rows, 1)
    smoothed = (
        centre + spread_y * laplace(with_rim, 1) + spread_x * laplace(pad_along(centre), 2)
    ) * transparency
    flat_cells = smoothed.reshape(local_comps, -1)
    sea_cells = sea_order.reshape(-1)[:SEA_MAX]
    columns = flat_cells.at[:, sea_cells].get(mode="promise_in_bounds", unique_indices=True)
    gathered = lax.all_to_all(columns, "spec", split_axis=1, concat_axis=0, tiled=True)
    source_terms = interact_pallas(gathered, coupling, quad_offsets)
    returned = lax.all_to_all(source_terms, "spec", split_axis=0, concat_axis=1, tiled=True)
    new_cells = flat_cells.at[:, sea_cells].add(
        returned, mode="promise_in_bounds", unique_indices=True
    )
    updated = new_cells.reshape(smoothed.shape)
    return (updated, source_terms.astype(jnp.bfloat16)[None])


def solution(mesh):
    in_specs = (
        P("spec", "lat", "groups"),
        P("lat", "groups"),
        P("lat", "groups"),
        P(),
        P(),
        P(),
        P(),
    )
    out_specs = (P("spec", "lat", "groups"), P(("groups", "lat"), None, "spec"))
    return jax.shard_map(
        on_device, mesh=mesh, in_specs=in_specs, out_specs=out_specs, check_vma=False
    )
```

```python
import math

import jax
import jax.numpy as jnp
from jax import lax
from jax.experimental import pallas as pl
from jax.experimental.pallas import tpu as pltpu
from jax.sharding import PartitionSpec as P

NDIR = 36
NFREQ = 32
SUBSTEPS = 2
SEA_MAX = 3072


gain_up = 1.25 ** (-4)
gain_down = 0.75 ** (-4)
gain_cross = 0.9375 ** (-4)


def border_rows(block, axis, dim, width):
    count = lax.axis_size(axis)
    bottom = lax.slice_in_dim(block, block.shape[dim] - width, None, axis=dim)
    top = lax.slice_in_dim(block, 0, width, axis=dim)
    if count == 2:
        first = lax.axis_index(axis) == 0
        swapped = lax.ppermute(jnp.where(first, bottom, top), axis, [(0, 1), (1, 0)])
        return jnp.where(first, 0.0, swapped), jnp.where(first, swapped, 0.0)
    forward = [(i, i + 1) for i in range(count - 1)]
    backward = [(target, source) for source, target in forward]
    return lax.ppermute(bottom, axis, forward), lax.ppermute(top, axis, backward)


def cut_slab(values, offset, length, along):
    return lax.slice_in_dim(values, offset, offset + length, axis=along)


def pad_along(values):
    return jnp.pad(values, ((0, 0), (0, 0), (2, 2)))


def quickest(padded, courant, along):
    length = padded.shape[along] - 4
    before_cell = cut_slab(padded, 0, length + 1, along)
    left_cell = cut_slab(padded, 1, length + 1, along)
    right_cell = cut_slab(padded, 2, length + 1, along)
    after_cell = cut_slab(padded, 3, length + 1, along)
    curvature = jnp.where(
        courant > 0,
        right_cell - 2.0 * left_cell + before_cell,
        after_cell - 2.0 * right_cell + left_cell,
    )
    face_value = (
        0.5 * (left_cell + right_cell)
        - 0.5 * courant * (right_cell - left_cell)
        - (1.0 - courant * courant) / 6.0 * curvature
    )
    face_flux = courant * face_value
    return cut_slab(padded, 2, length, along) - (
        cut_slab(face_flux, 1, length, along) - cut_slab(face_flux, 0, length, along)
    )


def laplace(padded, along):
    length = padded.shape[along] - 4
    centre = cut_slab(padded, 2, length, along)
    near_sum = (
        cut_slab(padded, 1, length, along) + cut_slab(padded, 3, length, along) - 2.0 * centre
    )
    far_sum = cut_slab(padded, 0, length, along) + cut_slab(padded, 4, length, along) - 2.0 * centre
    return 4.0 / 3.0 * near_sum - 1.0 / 12.0 * far_sum


def interact_kernel(off_ref, w_ref, e_ref, s_ref, t_ref):
    up_freq = off_ref[0]
    down_freq = off_ref[1]
    dir_one = off_ref[2]
    dir_two = off_ref[3]
    weight = w_ref[...]
    up_shift = (NFREQ - up_freq) % NFREQ
    down_shift = down_freq % NFREQ

    def transfers(d, carry):
        spectra = e_ref[d]
        squared = spectra * spectra
        for slot, mirror in enumerate((1, -1)):
            upper_bin = pltpu.roll(e_ref[(d + mirror * dir_one) % NDIR], up_shift, 0)
            lower_bin = pltpu.roll(e_ref[(d - mirror * dir_two) % NDIR], down_shift, 0)
            t_ref[slot, d] = weight * (
                squared * (upper_bin * gain_up + lower_bin * gain_down)
                - 2.0 * gain_cross * spectra * upper_bin * lower_bin
            )
        return carry

    lax.fori_loop(0, NDIR, transfers, 0)

    def sources(d, carry):
        total = -2.0 * t_ref[0, d] - 2.0 * t_ref[1, d]
        for slot, mirror in enumerate((1, -1)):
            total = total + pltpu.roll(t_ref[slot, (d - mirror * dir_one) % NDIR], up_freq % NFREQ, 0)
            total = total + pltpu.roll(
                t_ref[slot, (d + mirror * dir_two) % NDIR], (NFREQ - down_freq) % NFREQ, 0
            )
        s_ref[d] = total
        return carry

    lax.fori_loop(0, NDIR, sources, 0)


def interact_pallas(columns, coupling, quad_offsets):
    comps, points = columns.shape
    spectra = columns.reshape(NFREQ, NDIR, points).transpose(1, 0, 2)
    freq_index = lax.iota(jnp.int32, NFREQ)
    inside = ((freq_index + quad_offsets[0] < NFREQ) & (freq_index - quad_offsets[1] >= 0)).astype(jnp.float32)
    weight = (coupling * inside)[:, None]
    out = pl.pallas_call(
        interact_kernel,
        out_shape=jax.ShapeDtypeStruct((NDIR, NFREQ, points), jnp.float32),
        in_specs=[
            pl.BlockSpec(memory_space=pltpu.SMEM),
            pl.BlockSpec(memory_space=pltpu.VMEM),
            pl.BlockSpec(memory_space=pltpu.VMEM),
        ],
        out_specs=pl.BlockSpec(memory_space=pltpu.VMEM),
        scratch_shapes=[pltpu.VMEM((2, NDIR, NFREQ, points), jnp.float32)],
    )(quad_offsets, weight, spectra)
    return out.transpose(1, 0, 2).reshape(comps, points)


def per_component(lookup, freq_index):
    matches = freq_index[:, None] == lax.iota(jnp.int32, lookup.shape[0])[None, :]
    return jnp.sum(jnp.where(matches, lookup[None, :], 0.0), axis=1)


def propagate(energy, ext_mask, courant_y, courant_x):
    for substep in range(SUBSTEPS):
        energy = quickest(energy, courant_y, 1)
        ext_mask = cut_slab(ext_mask, 2, ext_mask.shape[0] - 4, 0)
        energy = quickest(pad_along(energy), courant_x, 2) * ext_mask
    return energy


def on_device(spectrum, transparency, sea_order, speeds, sprinkle, coupling, quad_offsets):
    local_comps = spectrum.shape[0]
    band_rows = spectrum.shape[1]
    first_comp = lax.axis_index("spec") * local_comps
    comp_index = first_comp + lax.iota(jnp.int32, local_comps)
    freq_index = comp_index // NDIR
    dir_index = comp_index % NDIR
    angles = 2.0 * math.pi * (dir_index.astype(jnp.float32) + 0.5) / NDIR
    sines = jnp.sin(angles)
    cosines = jnp.cos(angles)
    speed_comp = per_component(speeds, freq_index)
    spread = per_component(sprinkle, freq_index)
    courant_y = (speed_comp * sines)[:, None, None]
    courant_x = (speed_comp * cosines)[:, None, None]
    spread_y = (spread * (sines * sines + 0.25 * cosines * cosines))[:, None, None]
    spread_x = (spread * (cosines * cosines + 0.25 * sines * sines))[:, None, None]
    stacked = jnp.concatenate([transparency[None], spectrum], axis=0)
    width = 2 * SUBSTEPS + 2

    def smooth_window(window):
        rows = window.shape[1] - 2 * width
        with_rim = propagate(window[1:], window[0], courant_y, courant_x)
        centre = cut_slab(with_rim, 2, rows, 1)
        return (
            centre + spread_y * laplace(with_rim, 1) + spread_x * laplace(pad_along(centre), 2)
        ) * cut_slab(window[0], width, rows, 0)

    low, high = border_rows(stacked, "lat", 1, width)
    if band_rows > 2 * width:
        inner = smooth_window(stacked)
        top = smooth_window(jnp.concatenate([low, stacked[:, : 2 * width]], axis=1))
        bottom = smooth_window(jnp.concatenate([stacked[:, band_rows - 2 * width :], high], axis=1))
        smoothed = jnp.concatenate([top, inner, bottom], axis=1)
    else:
        smoothed = smooth_window(jnp.concatenate([low, stacked, high], axis=1))
    flat_cells = smoothed.reshape(local_comps, -1)
    sea_cells = sea_order.reshape(-1)[:SEA_MAX]
    columns = flat_cells.at[:, sea_cells].get(mode="promise_in_bounds", unique_indices=True)
    gathered = lax.all_to_all(columns, "spec", split_axis=1, concat_axis=0, tiled=True)
    source_terms = interact_pallas(gathered, coupling, quad_offsets)
    returned = lax.all_to_all(source_terms, "spec", split_axis=0, concat_axis=1, tiled=True)
    new_cells = flat_cells.at[:, sea_cells].add(
        returned, mode="promise_in_bounds", unique_indices=True
    )
    updated = new_cells.reshape(smoothed.shape)
    return (updated, source_terms.astype(jnp.bfloat16)[None])


def solution(mesh):
    in_specs = (
        P("spec", "lat", "groups"),
        P("lat", "groups"),
        P("lat", "groups"),
        P(),
        P(),
        P(),
        P(),
    )
    out_specs = (P("spec", "lat", "groups"), P(("groups", "lat"), None, "spec"))
    return jax.shard_map(
        on_device, mesh=mesh, in_specs=in_specs, out_specs=out_specs, check_vma=False
    )
```

```python
import math

import jax
import jax.numpy as jnp
from jax import lax
from jax.experimental import pallas as pl
from jax.experimental.pallas import tpu as pltpu
from jax.sharding import PartitionSpec as P

NDIR = 36
NFREQ = 32
SUBSTEPS = 2
SEA_MAX = 3072


gain_up = 1.25 ** (-4)
gain_down = 0.75 ** (-4)
gain_cross = 0.9375 ** (-4)


def extended_2(block, sides, width):
    for axis, dim in sides:
        count = lax.axis_size(axis)
        bottom = lax.slice_in_dim(block, block.shape[dim] - width, None, axis=dim)
        top = lax.slice_in_dim(block, 0, width, axis=dim)
        if count == 2:
            first = lax.axis_index(axis) == 0
            swapped = lax.ppermute(jnp.where(first, bottom, top), axis, [(0, 1), (1, 0)])
            low = jnp.where(first, 0.0, swapped)
            high = jnp.where(first, swapped, 0.0)
        else:
            forward = [(i, i + 1) for i in range(count - 1)]
            backward = [(target, source) for source, target in forward]
            low = lax.ppermute(bottom, axis, forward)
            high = lax.ppermute(top, axis, backward)
        block = jnp.concatenate([low, block, high], axis=dim)
    return block


def cut_slab(values, offset, length, along):
    return lax.slice_in_dim(values, offset, offset + length, axis=along)


def quickest(padded, courant, along):
    length = padded.shape[along] - 4
    before_cell = cut_slab(padded, 0, length + 1, along)
    left_cell = cut_slab(padded, 1, length + 1, along)
    right_cell = cut_slab(padded, 2, length + 1, along)
    after_cell = cut_slab(padded, 3, length + 1, along)
    curvature = jnp.where(
        courant > 0,
        right_cell - 2.0 * left_cell + before_cell,
        after_cell - 2.0 * right_cell + left_cell,
    )
    face_value = (
        0.5 * (left_cell + right_cell)
        - 0.5 * courant * (right_cell - left_cell)
        - (1.0 - courant * courant) / 6.0 * curvature
    )
    face_flux = courant * face_value
    return cut_slab(padded, 2, length, along) - (
        cut_slab(face_flux, 1, length, along) - cut_slab(face_flux, 0, length, along)
    )


def shifted(values, offset, along):
    config = [(0, 0, 0)] * values.ndim
    config[along] = (offset, -offset, 0)
    return lax.pad(values, jnp.zeros((), values.dtype), config)


def face_flux(before_cell, left_cell, right_cell, after_cell, courant):
    curvature = jnp.where(
        courant > 0,
        right_cell - 2.0 * left_cell + before_cell,
        after_cell - 2.0 * right_cell + left_cell,
    )
    face_value = (
        0.5 * (left_cell + right_cell)
        - 0.5 * courant * (right_cell - left_cell)
        - (1.0 - courant * courant) / 6.0 * curvature
    )
    return courant * face_value


def quickest_x(energy, courant):
    back_two = shifted(energy, 2, 2)
    back_one = shifted(energy, 1, 2)
    ahead_one = shifted(energy, -1, 2)
    ahead_two = shifted(energy, -2, 2)
    right_face = face_flux(back_one, energy, ahead_one, ahead_two, courant)
    left_face = face_flux(back_two, back_one, energy, ahead_one, courant)
    return energy - (right_face - left_face)


def laplace_x(centre):
    near_sum = shifted(centre, 1, 2) + shifted(centre, -1, 2) - 2.0 * centre
    far_sum = shifted(centre, 2, 2) + shifted(centre, -2, 2) - 2.0 * centre
    return 4.0 / 3.0 * near_sum - 1.0 / 12.0 * far_sum


def laplace(padded, along):
    length = padded.shape[along] - 4
    centre = cut_slab(padded, 2, length, along)
    near_sum = (
        cut_slab(padded, 1, length, along) + cut_slab(padded, 3, length, along) - 2.0 * centre
    )
    far_sum = cut_slab(padded, 0, length, along) + cut_slab(padded, 4, length, along) - 2.0 * centre
    return 4.0 / 3.0 * near_sum - 1.0 / 12.0 * far_sum


def interact_kernel(off_ref, w_ref, e_ref, s_ref, t_ref):
    up_freq = off_ref[0]
    down_freq = off_ref[1]
    dir_one = off_ref[2]
    dir_two = off_ref[3]
    weight = w_ref[...]
    up_shift = (NFREQ - up_freq) % NFREQ
    down_shift = down_freq % NFREQ

    def transfers(d, carry):
        spectra = e_ref[d]
        squared = spectra * spectra
        for slot, mirror in enumerate((1, -1)):
            upper_bin = pltpu.roll(e_ref[(d + mirror * dir_one) % NDIR], up_shift, 0)
            lower_bin = pltpu.roll(e_ref[(d - mirror * dir_two) % NDIR], down_shift, 0)
            t_ref[slot, d] = weight * (
                squared * (upper_bin * gain_up + lower_bin * gain_down)
                - 2.0 * gain_cross * spectra * upper_bin * lower_bin
            )
        return carry

    lax.fori_loop(0, NDIR, transfers, 0)

    def sources(d, carry):
        total = -2.0 * t_ref[0, d] - 2.0 * t_ref[1, d]
        for slot, mirror in enumerate((1, -1)):
            total = total + pltpu.roll(t_ref[slot, (d - mirror * dir_one) % NDIR], up_freq % NFREQ, 0)
            total = total + pltpu.roll(
                t_ref[slot, (d + mirror * dir_two) % NDIR], (NFREQ - down_freq) % NFREQ, 0
            )
        s_ref[d] = total
        return carry

    lax.fori_loop(0, NDIR, sources, 0)


def interact_pallas(columns, coupling, quad_offsets):
    comps, points = columns.shape
    spectra = columns.reshape(NFREQ, NDIR, points).transpose(1, 0, 2)
    freq_index = lax.iota(jnp.int32, NFREQ)
    inside = ((freq_index + quad_offsets[0] < NFREQ) & (freq_index - quad_offsets[1] >= 0)).astype(jnp.float32)
    weight = (coupling * inside)[:, None]
    out = pl.pallas_call(
        interact_kernel,
        out_shape=jax.ShapeDtypeStruct((NDIR, NFREQ, points), jnp.float32),
        in_specs=[
            pl.BlockSpec(memory_space=pltpu.SMEM),
            pl.BlockSpec(memory_space=pltpu.VMEM),
            pl.BlockSpec(memory_space=pltpu.VMEM),
        ],
        out_specs=pl.BlockSpec(memory_space=pltpu.VMEM),
        scratch_shapes=[pltpu.VMEM((2, NDIR, NFREQ, points), jnp.float32)],
    )(quad_offsets, weight, spectra)
    return out.transpose(1, 0, 2).reshape(comps, points)


def per_component(lookup, freq_index):
    matches = freq_index[:, None] == lax.iota(jnp.int32, lookup.shape[0])[None, :]
    return jnp.sum(jnp.where(matches, lookup[None, :], 0.0), axis=1)


def propagate(energy, ext_mask, courant_y, courant_x):
    for substep in range(SUBSTEPS):
        energy = quickest(energy, courant_y, 1)
        ext_mask = cut_slab(ext_mask, 2, ext_mask.shape[0] - 4, 0)
        energy = quickest_x(energy, courant_x) * ext_mask
    return energy


def on_device(spectrum, transparency, sea_order, speeds, sprinkle, coupling, quad_offsets):
    local_comps = spectrum.shape[0]
    band_rows = spectrum.shape[1]
    first_comp = lax.axis_index("spec") * local_comps
    comp_index = first_comp + lax.iota(jnp.int32, local_comps)
    freq_index = comp_index // NDIR
    dir_index = comp_index % NDIR
    angles = 2.0 * math.pi * (dir_index.astype(jnp.float32) + 0.5) / NDIR
    sines = jnp.sin(angles)
    cosines = jnp.cos(angles)
    speed_comp = per_component(speeds, freq_index)
    spread = per_component(sprinkle, freq_index)
    courant_y = (speed_comp * sines)[:, None, None]
    courant_x = (speed_comp * cosines)[:, None, None]
    spread_y = (spread * (sines * sines + 0.25 * cosines * cosines))[:, None, None]
    spread_x = (spread * (cosines * cosines + 0.25 * sines * sines))[:, None, None]
    stacked = jnp.concatenate([transparency[None], spectrum], axis=0)
    reach = 2 * SUBSTEPS
    extended = extended_2(stacked, (("lat", 1),), reach + 2)
    with_rim = propagate(extended[1:], extended[0], courant_y, courant_x)
    centre = cut_slab(with_rim, 2, band_rows, 1)
    smoothed = (
        centre + spread_y * laplace(with_rim, 1) + spread_x * laplace_x(centre)
    ) * transparency
    flat_cells = smoothed.reshape(local_comps, -1)
    sea_cells = sea_order.reshape(-1)[:SEA_MAX]
    columns = flat_cells.at[:, sea_cells].get(mode="promise_in_bounds", unique_indices=True)
    gathered = lax.all_to_all(columns, "spec", split_axis=1, concat_axis=0, tiled=True)
    source_terms = interact_pallas(gathered, coupling, quad_offsets)
    returned = lax.all_to_all(source_terms, "spec", split_axis=0, concat_axis=1, tiled=True)
    new_cells = flat_cells.at[:, sea_cells].add(
        returned, mode="promise_in_bounds", unique_indices=True
    )
    updated = new_cells.reshape(smoothed.shape)
    return (updated, source_terms.astype(jnp.bfloat16)[None])


def solution(mesh):
    in_specs = (
        P("spec", "lat", "groups"),
        P("lat", "groups"),
        P("lat", "groups"),
        P(),
        P(),
        P(),
        P(),
    )
    out_specs = (P("spec", "lat", "groups"), P(("groups", "lat"), None, "spec"))
    return jax.shard_map(
        on_device, mesh=mesh, in_specs=in_specs, out_specs=out_specs, check_vma=False
    )
```

```python
import math

import jax
import jax.numpy as jnp
from jax import lax
from jax.experimental import pallas as pl
from jax.experimental.pallas import tpu as pltpu
from jax.sharding import PartitionSpec as P

NDIR = 36
NFREQ = 32
SUBSTEPS = 2
SEA_MAX = 3072


gain_up = 1.25 ** (-4)
gain_down = 0.75 ** (-4)
gain_cross = 0.9375 ** (-4)


def extended_2(block, sides, width):
    for axis, dim in sides:
        count = lax.axis_size(axis)
        bottom = lax.slice_in_dim(block, block.shape[dim] - width, None, axis=dim)
        top = lax.slice_in_dim(block, 0, width, axis=dim)
        if count == 2:
            first = lax.axis_index(axis) == 0
            swapped = lax.ppermute(jnp.where(first, bottom, top), axis, [(0, 1), (1, 0)])
            low = jnp.where(first, 0.0, swapped)
            high = jnp.where(first, swapped, 0.0)
        else:
            forward = [(i, i + 1) for i in range(count - 1)]
            backward = [(target, source) for source, target in forward]
            low = lax.ppermute(bottom, axis, forward)
            high = lax.ppermute(top, axis, backward)
        block = jnp.concatenate([low, block, high], axis=dim)
    return block


def cut_slab(values, offset, length, along):
    return lax.slice_in_dim(values, offset, offset + length, axis=along)


def shifted(values, offset, along):
    config = [(0, 0, 0)] * values.ndim
    config[along] = (offset, -offset, 0)
    return lax.pad(values, jnp.zeros((), values.dtype), config)


def face_flux(before_cell, left_cell, right_cell, after_cell, courant):
    curvature = jnp.where(
        courant > 0,
        right_cell - 2.0 * left_cell + before_cell,
        after_cell - 2.0 * right_cell + left_cell,
    )
    face_value = (
        0.5 * (left_cell + right_cell)
        - 0.5 * courant * (right_cell - left_cell)
        - (1.0 - courant * courant) / 6.0 * curvature
    )
    return courant * face_value


def quickest_x(energy, courant):
    back_two = shifted(energy, 2, 2)
    back_one = shifted(energy, 1, 2)
    ahead_one = shifted(energy, -1, 2)
    ahead_two = shifted(energy, -2, 2)
    right_face = face_flux(back_one, energy, ahead_one, ahead_two, courant)
    left_face = face_flux(back_two, back_one, energy, ahead_one, courant)
    return energy - (right_face - left_face)


def quickest_rows(padded, courant):
    length = padded.shape[1] - 4
    cells = [cut_slab(padded, offset, length, 1) for offset in range(5)]
    right_face = face_flux(cells[1], cells[2], cells[3], cells[4], courant)
    left_face = face_flux(cells[0], cells[1], cells[2], cells[3], courant)
    return cells[2] - (right_face - left_face)


def laplace_x(centre):
    near_sum = shifted(centre, 1, 2) + shifted(centre, -1, 2) - 2.0 * centre
    far_sum = shifted(centre, 2, 2) + shifted(centre, -2, 2) - 2.0 * centre
    return 4.0 / 3.0 * near_sum - 1.0 / 12.0 * far_sum


def laplace(padded, along):
    length = padded.shape[along] - 4
    centre = cut_slab(padded, 2, length, along)
    near_sum = (
        cut_slab(padded, 1, length, along) + cut_slab(padded, 3, length, along) - 2.0 * centre
    )
    far_sum = cut_slab(padded, 0, length, along) + cut_slab(padded, 4, length, along) - 2.0 * centre
    return 4.0 / 3.0 * near_sum - 1.0 / 12.0 * far_sum


def interact_kernel(off_ref, w_ref, e_ref, s_ref, t_ref):
    up_freq = off_ref[0]
    down_freq = off_ref[1]
    dir_one = off_ref[2]
    dir_two = off_ref[3]
    weight = w_ref[...]
    up_shift = (NFREQ - up_freq) % NFREQ
    down_shift = down_freq % NFREQ

    def transfers(d, carry):
        spectra = e_ref[d]
        squared = spectra * spectra
        for slot, mirror in enumerate((1, -1)):
            upper_bin = pltpu.roll(e_ref[(d + mirror * dir_one) % NDIR], up_shift, 0)
            lower_bin = pltpu.roll(e_ref[(d - mirror * dir_two) % NDIR], down_shift, 0)
            t_ref[slot, d] = weight * (
                squared * (upper_bin * gain_up + lower_bin * gain_down)
                - 2.0 * gain_cross * spectra * upper_bin * lower_bin
            )
        return carry

    lax.fori_loop(0, NDIR, transfers, 0)

    def sources(d, carry):
        total = -2.0 * t_ref[0, d] - 2.0 * t_ref[1, d]
        for slot, mirror in enumerate((1, -1)):
            total = total + pltpu.roll(t_ref[slot, (d - mirror * dir_one) % NDIR], up_freq % NFREQ, 0)
            total = total + pltpu.roll(
                t_ref[slot, (d + mirror * dir_two) % NDIR], (NFREQ - down_freq) % NFREQ, 0
            )
        s_ref[d] = total
        return carry

    lax.fori_loop(0, NDIR, sources, 0)


def interact_pallas(columns, coupling, quad_offsets):
    comps, points = columns.shape
    spectra = columns.reshape(NFREQ, NDIR, points).transpose(1, 0, 2)
    freq_index = lax.iota(jnp.int32, NFREQ)
    inside = ((freq_index + quad_offsets[0] < NFREQ) & (freq_index - quad_offsets[1] >= 0)).astype(jnp.float32)
    weight = (coupling * inside)[:, None]
    out = pl.pallas_call(
        interact_kernel,
        out_shape=jax.ShapeDtypeStruct((NDIR, NFREQ, points), jnp.float32),
        in_specs=[
            pl.BlockSpec(memory_space=pltpu.SMEM),
            pl.BlockSpec(memory_space=pltpu.VMEM),
            pl.BlockSpec(memory_space=pltpu.VMEM),
        ],
        out_specs=pl.BlockSpec(memory_space=pltpu.VMEM),
        scratch_shapes=[pltpu.VMEM((2, NDIR, NFREQ, points), jnp.float32)],
    )(quad_offsets, weight, spectra)
    return out.transpose(1, 0, 2).reshape(comps, points)


def per_component(lookup, freq_index):
    matches = freq_index[:, None] == lax.iota(jnp.int32, lookup.shape[0])[None, :]
    return jnp.sum(jnp.where(matches, lookup[None, :], 0.0), axis=1)


def propagate(energy, ext_mask, courant_y, courant_x):
    for substep in range(SUBSTEPS):
        energy = quickest_rows(energy, courant_y)
        ext_mask = cut_slab(ext_mask, 2, ext_mask.shape[0] - 4, 0)
        energy = quickest_x(energy, courant_x) * ext_mask
    return energy


def on_device(spectrum, transparency, sea_order, speeds, sprinkle, coupling, quad_offsets):
    local_comps = spectrum.shape[0]
    band_rows = spectrum.shape[1]
    first_comp = lax.axis_index("spec") * local_comps
    comp_index = first_comp + lax.iota(jnp.int32, local_comps)
    freq_index = comp_index // NDIR
    dir_index = comp_index % NDIR
    angles = 2.0 * math.pi * (dir_index.astype(jnp.float32) + 0.5) / NDIR
    sines = jnp.sin(angles)
    cosines = jnp.cos(angles)
    speed_comp = per_component(speeds, freq_index)
    spread = per_component(sprinkle, freq_index)
    courant_y = (speed_comp * sines)[:, None, None]
    courant_x = (speed_comp * cosines)[:, None, None]
    spread_y = (spread * (sines * sines + 0.25 * cosines * cosines))[:, None, None]
    spread_x = (spread * (cosines * cosines + 0.25 * sines * sines))[:, None, None]
    stacked = jnp.concatenate([transparency[None], spectrum], axis=0)
    reach = 2 * SUBSTEPS
    extended = extended_2(stacked, (("lat", 1),), reach + 2)
    with_rim = propagate(extended[1:], extended[0], courant_y, courant_x)
    centre = cut_slab(with_rim, 2, band_rows, 1)
    smoothed = (
        centre + spread_y * laplace(with_rim, 1) + spread_x * laplace_x(centre)
    ) * transparency
    flat_cells = smoothed.reshape(local_comps, -1)
    sea_cells = sea_order.reshape(-1)[:SEA_MAX]
    columns = flat_cells.at[:, sea_cells].get(mode="promise_in_bounds", unique_indices=True)
    gathered = lax.all_to_all(columns, "spec", split_axis=1, concat_axis=0, tiled=True)
    source_terms = interact_pallas(gathered, coupling, quad_offsets)
    returned = lax.all_to_all(source_terms, "spec", split_axis=0, concat_axis=1, tiled=True)
    new_cells = flat_cells.at[:, sea_cells].add(
        returned, mode="promise_in_bounds", unique_indices=True
    )
    updated = new_cells.reshape(smoothed.shape)
    return (updated, source_terms.astype(jnp.bfloat16)[None])


def solution(mesh):
    in_specs = (
        P("spec", "lat", "groups"),
        P("lat", "groups"),
        P("lat", "groups"),
        P(),
        P(),
        P(),
        P(),
    )
    out_specs = (P("spec", "lat", "groups"), P(("groups", "lat"), None, "spec"))
    return jax.shard_map(
        on_device, mesh=mesh, in_specs=in_specs, out_specs=out_specs, check_vma=False
    )
```

```python
import math

import jax
import jax.numpy as jnp
from jax import lax
from jax.experimental import pallas as pl
from jax.experimental.pallas import tpu as pltpu
from jax.sharding import PartitionSpec as P

NDIR = 36
NFREQ = 32
SUBSTEPS = 2
SEA_MAX = 3072


gain_up = 1.25 ** (-4)
gain_down = 0.75 ** (-4)
gain_cross = 0.9375 ** (-4)


def extended_2(block, sides, width):
    for axis, dim in sides:
        count = lax.axis_size(axis)
        bottom = lax.slice_in_dim(block, block.shape[dim] - width, None, axis=dim)
        top = lax.slice_in_dim(block, 0, width, axis=dim)
        if count == 2:
            first = lax.axis_index(axis) == 0
            swapped = lax.ppermute(jnp.where(first, bottom, top), axis, [(0, 1), (1, 0)])
            low = jnp.where(first, 0.0, swapped)
            high = jnp.where(first, swapped, 0.0)
        else:
            forward = [(i, i + 1) for i in range(count - 1)]
            backward = [(target, source) for source, target in forward]
            low = lax.ppermute(bottom, axis, forward)
            high = lax.ppermute(top, axis, backward)
        block = jnp.concatenate([low, block, high], axis=dim)
    return block


def cut_slab(values, offset, length, along):
    return lax.slice_in_dim(values, offset, offset + length, axis=along)


def quickest(padded, courant, along):
    length = padded.shape[along] - 4
    before_cell = cut_slab(padded, 0, length + 1, along)
    left_cell = cut_slab(padded, 1, length + 1, along)
    right_cell = cut_slab(padded, 2, length + 1, along)
    after_cell = cut_slab(padded, 3, length + 1, along)
    curvature = jnp.where(
        courant > 0,
        right_cell - 2.0 * left_cell + before_cell,
        after_cell - 2.0 * right_cell + left_cell,
    )
    face_value = (
        0.5 * (left_cell + right_cell)
        - 0.5 * courant * (right_cell - left_cell)
        - (1.0 - courant * courant) / 6.0 * curvature
    )
    face_flux = courant * face_value
    return cut_slab(padded, 2, length, along) - (
        cut_slab(face_flux, 1, length, along) - cut_slab(face_flux, 0, length, along)
    )


def shifted(values, offset, along):
    config = [(0, 0, 0)] * values.ndim
    config[along] = (offset, -offset, 0)
    return lax.pad(values, jnp.zeros((), values.dtype), config)


def face_flux(before_cell, left_cell, right_cell, after_cell, courant):
    curvature = jnp.where(
        courant > 0,
        right_cell - 2.0 * left_cell + before_cell,
        after_cell - 2.0 * right_cell + left_cell,
    )
    face_value = (
        0.5 * (left_cell + right_cell)
        - 0.5 * courant * (right_cell - left_cell)
        - (1.0 - courant * courant) / 6.0 * curvature
    )
    return courant * face_value


def quickest_x(energy, courant):
    back_two = shifted(energy, 2, 2)
    back_one = shifted(energy, 1, 2)
    ahead_one = shifted(energy, -1, 2)
    ahead_two = shifted(energy, -2, 2)
    right_face = face_flux(back_one, energy, ahead_one, ahead_two, courant)
    left_face = face_flux(back_two, back_one, energy, ahead_one, courant)
    return energy - (right_face - left_face)


def laplace_x(centre):
    near_sum = shifted(centre, 1, 2) + shifted(centre, -1, 2) - 2.0 * centre
    far_sum = shifted(centre, 2, 2) + shifted(centre, -2, 2) - 2.0 * centre
    return 4.0 / 3.0 * near_sum - 1.0 / 12.0 * far_sum


def laplace(padded, along):
    length = padded.shape[along] - 4
    centre = cut_slab(padded, 2, length, along)
    near_sum = (
        cut_slab(padded, 1, length, along) + cut_slab(padded, 3, length, along) - 2.0 * centre
    )
    far_sum = cut_slab(padded, 0, length, along) + cut_slab(padded, 4, length, along) - 2.0 * centre
    return 4.0 / 3.0 * near_sum - 1.0 / 12.0 * far_sum


def interact_kernel(off_ref, w_ref, e_ref, s_ref, t_ref):
    up_freq = off_ref[0]
    down_freq = off_ref[1]
    dir_one = off_ref[2]
    dir_two = off_ref[3]
    weight = w_ref[...]
    up_shift = (NFREQ - up_freq) % NFREQ
    down_shift = down_freq % NFREQ

    def transfers(d, carry):
        spectra = e_ref[d]
        squared = spectra * spectra
        for slot, mirror in enumerate((1, -1)):
            upper_bin = pltpu.roll(e_ref[(d + mirror * dir_one) % NDIR], up_shift, 0)
            lower_bin = pltpu.roll(e_ref[(d - mirror * dir_two) % NDIR], down_shift, 0)
            t_ref[slot, d] = weight * (
                squared * (upper_bin * gain_up + lower_bin * gain_down)
                - 2.0 * gain_cross * spectra * upper_bin * lower_bin
            )
        return carry

    lax.fori_loop(0, NDIR, transfers, 0)

    def sources(d, carry):
        total = -2.0 * t_ref[0, d] - 2.0 * t_ref[1, d]
        for slot, mirror in enumerate((1, -1)):
            total = total + pltpu.roll(t_ref[slot, (d - mirror * dir_one) % NDIR], up_freq % NFREQ, 0)
            total = total + pltpu.roll(
                t_ref[slot, (d + mirror * dir_two) % NDIR], (NFREQ - down_freq) % NFREQ, 0
            )
        s_ref[d] = total
        return carry

    lax.fori_loop(0, NDIR, sources, 0)


def interact_pallas(columns, coupling, quad_offsets):
    comps, points = columns.shape
    spectra = columns.reshape(NFREQ, NDIR, points).transpose(1, 0, 2)
    freq_index = lax.iota(jnp.int32, NFREQ)
    inside = ((freq_index + quad_offsets[0] < NFREQ) & (freq_index - quad_offsets[1] >= 0)).astype(jnp.float32)
    weight = (coupling * inside)[:, None]
    out = pl.pallas_call(
        interact_kernel,
        out_shape=jax.ShapeDtypeStruct((NDIR, NFREQ, points), jnp.float32),
        in_specs=[
            pl.BlockSpec(memory_space=pltpu.SMEM),
            pl.BlockSpec(memory_space=pltpu.VMEM),
            pl.BlockSpec(memory_space=pltpu.VMEM),
        ],
        out_specs=pl.BlockSpec(memory_space=pltpu.VMEM),
        scratch_shapes=[pltpu.VMEM((2, NDIR, NFREQ, points), jnp.float32)],
    )(quad_offsets, weight, spectra)
    return out.transpose(1, 0, 2).reshape(comps, points)


def per_component(lookup, freq_index):
    matches = freq_index[:, None] == lax.iota(jnp.int32, lookup.shape[0])[None, :]
    return jnp.sum(jnp.where(matches, lookup[None, :], 0.0), axis=1)


def propagate(energy, ext_mask, courant_y, courant_x):
    for substep in range(SUBSTEPS):
        energy = quickest(energy, courant_y, 1)
        ext_mask = cut_slab(ext_mask, 2, ext_mask.shape[0] - 4, 0)
        energy = quickest_x(energy, courant_x) * ext_mask
    return energy


def on_device(spectrum, transparency, sea_order, speeds, sprinkle, coupling, quad_offsets):
    local_comps = spectrum.shape[0]
    band_rows = spectrum.shape[1]
    first_comp = lax.axis_index("spec") * local_comps
    comp_index = first_comp + lax.iota(jnp.int32, local_comps)
    freq_index = comp_index // NDIR
    dir_index = comp_index % NDIR
    angles = 2.0 * math.pi * (dir_index.astype(jnp.float32) + 0.5) / NDIR
    sines = jnp.sin(angles)
    cosines = jnp.cos(angles)
    speed_comp = per_component(speeds, freq_index)
    spread = per_component(sprinkle, freq_index)
    courant_y = (speed_comp * sines)[:, None, None]
    courant_x = (speed_comp * cosines)[:, None, None]
    spread_y = (spread * (sines * sines + 0.25 * cosines * cosines))[:, None, None]
    spread_x = (spread * (cosines * cosines + 0.25 * sines * sines))[:, None, None]
    width = 2 * SUBSTEPS + 2
    split = local_comps // 2 if local_comps % 2 == 0 else local_comps
    parts = [
        jnp.concatenate([transparency[None], spectrum[start : start + split]], axis=0)
        for start in range(0, local_comps, split)
    ]
    extended = [extended_2(part, (("lat", 1),), width) for part in parts]
    pieces = []
    start = 0
    for part in extended:
        stop = start + part.shape[0] - 1
        with_rim = propagate(part[1:], part[0], courant_y[start:stop], courant_x[start:stop])
        centre = cut_slab(with_rim, 2, band_rows, 1)
        pieces.append(
            (
                centre
                + spread_y[start:stop] * laplace(with_rim, 1)
                + spread_x[start:stop] * laplace_x(centre)
            )
            * transparency
        )
        start = stop
    smoothed = jnp.concatenate(pieces, axis=0)
    flat_cells = smoothed.reshape(local_comps, -1)
    sea_cells = sea_order.reshape(-1)[:SEA_MAX]
    columns = flat_cells.at[:, sea_cells].get(mode="promise_in_bounds", unique_indices=True)
    gathered = lax.all_to_all(columns, "spec", split_axis=1, concat_axis=0, tiled=True)
    source_terms = interact_pallas(gathered, coupling, quad_offsets)
    returned = lax.all_to_all(source_terms, "spec", split_axis=0, concat_axis=1, tiled=True)
    new_cells = flat_cells.at[:, sea_cells].add(
        returned, mode="promise_in_bounds", unique_indices=True
    )
    updated = new_cells.reshape(smoothed.shape)
    return (updated, source_terms.astype(jnp.bfloat16)[None])


def solution(mesh):
    in_specs = (
        P("spec", "lat", "groups"),
        P("lat", "groups"),
        P("lat", "groups"),
        P(),
        P(),
        P(),
        P(),
    )
    out_specs = (P("spec", "lat", "groups"), P(("groups", "lat"), None, "spec"))
    return jax.shard_map(
        on_device, mesh=mesh, in_specs=in_specs, out_specs=out_specs, check_vma=False
    )
```

```python
import math

import jax
import jax.numpy as jnp
from jax import lax
from jax.experimental import pallas as pl
from jax.experimental.pallas import tpu as pltpu
from jax.sharding import PartitionSpec as P

NDIR = 36
NFREQ = 32
SUBSTEPS = 2
SEA_MAX = 3072


gain_up = 1.25 ** (-4)
gain_down = 0.75 ** (-4)
gain_cross = 0.9375 ** (-4)


def border_rows(block, axis, dim, width):
    count = lax.axis_size(axis)
    bottom = lax.slice_in_dim(block, block.shape[dim] - width, None, axis=dim)
    top = lax.slice_in_dim(block, 0, width, axis=dim)
    if count == 2:
        first = lax.axis_index(axis) == 0
        swapped = lax.ppermute(jnp.where(first, bottom, top), axis, [(0, 1), (1, 0)])
        return jnp.where(first, 0.0, swapped), jnp.where(first, swapped, 0.0)
    forward = [(i, i + 1) for i in range(count - 1)]
    backward = [(target, source) for source, target in forward]
    return lax.ppermute(bottom, axis, forward), lax.ppermute(top, axis, backward)


def cut_slab(values, offset, length, along):
    return lax.slice_in_dim(values, offset, offset + length, axis=along)


def quickest(padded, courant, along):
    length = padded.shape[along] - 4
    before_cell = cut_slab(padded, 0, length + 1, along)
    left_cell = cut_slab(padded, 1, length + 1, along)
    right_cell = cut_slab(padded, 2, length + 1, along)
    after_cell = cut_slab(padded, 3, length + 1, along)
    curvature = jnp.where(
        courant > 0,
        right_cell - 2.0 * left_cell + before_cell,
        after_cell - 2.0 * right_cell + left_cell,
    )
    face_value = (
        0.5 * (left_cell + right_cell)
        - 0.5 * courant * (right_cell - left_cell)
        - (1.0 - courant * courant) / 6.0 * curvature
    )
    face_flux = courant * face_value
    return cut_slab(padded, 2, length, along) - (
        cut_slab(face_flux, 1, length, along) - cut_slab(face_flux, 0, length, along)
    )


def shifted(values, offset, along):
    config = [(0, 0, 0)] * values.ndim
    config[along] = (offset, -offset, 0)
    return lax.pad(values, jnp.zeros((), values.dtype), config)


def face_flux(before_cell, left_cell, right_cell, after_cell, courant):
    curvature = jnp.where(
        courant > 0,
        right_cell - 2.0 * left_cell + before_cell,
        after_cell - 2.0 * right_cell + left_cell,
    )
    face_value = (
        0.5 * (left_cell + right_cell)
        - 0.5 * courant * (right_cell - left_cell)
        - (1.0 - courant * courant) / 6.0 * curvature
    )
    return courant * face_value


def quickest_x(energy, courant):
    back_two = shifted(energy, 2, 2)
    back_one = shifted(energy, 1, 2)
    ahead_one = shifted(energy, -1, 2)
    ahead_two = shifted(energy, -2, 2)
    right_face = face_flux(back_one, energy, ahead_one, ahead_two, courant)
    left_face = face_flux(back_two, back_one, energy, ahead_one, courant)
    return energy - (right_face - left_face)


def laplace_x(centre):
    near_sum = shifted(centre, 1, 2) + shifted(centre, -1, 2) - 2.0 * centre
    far_sum = shifted(centre, 2, 2) + shifted(centre, -2, 2) - 2.0 * centre
    return 4.0 / 3.0 * near_sum - 1.0 / 12.0 * far_sum


def laplace(padded, along):
    length = padded.shape[along] - 4
    centre = cut_slab(padded, 2, length, along)
    near_sum = (
        cut_slab(padded, 1, length, along) + cut_slab(padded, 3, length, along) - 2.0 * centre
    )
    far_sum = cut_slab(padded, 0, length, along) + cut_slab(padded, 4, length, along) - 2.0 * centre
    return 4.0 / 3.0 * near_sum - 1.0 / 12.0 * far_sum


def interact_kernel(off_ref, w_ref, e_ref, s_ref, t_ref):
    up_freq = off_ref[0]
    down_freq = off_ref[1]
    dir_one = off_ref[2]
    dir_two = off_ref[3]
    weight = w_ref[...]
    up_shift = (NFREQ - up_freq) % NFREQ
    down_shift = down_freq % NFREQ

    def transfers(d, carry):
        spectra = e_ref[d]
        squared = spectra * spectra
        for slot, mirror in enumerate((1, -1)):
            upper_bin = pltpu.roll(e_ref[(d + mirror * dir_one) % NDIR], up_shift, 0)
            lower_bin = pltpu.roll(e_ref[(d - mirror * dir_two) % NDIR], down_shift, 0)
            t_ref[slot, d] = weight * (
                squared * (upper_bin * gain_up + lower_bin * gain_down)
                - 2.0 * gain_cross * spectra * upper_bin * lower_bin
            )
        return carry

    lax.fori_loop(0, NDIR, transfers, 0)

    def sources(d, carry):
        total = -2.0 * t_ref[0, d] - 2.0 * t_ref[1, d]
        for slot, mirror in enumerate((1, -1)):
            total = total + pltpu.roll(t_ref[slot, (d - mirror * dir_one) % NDIR], up_freq % NFREQ, 0)
            total = total + pltpu.roll(
                t_ref[slot, (d + mirror * dir_two) % NDIR], (NFREQ - down_freq) % NFREQ, 0
            )
        s_ref[d] = total
        return carry

    lax.fori_loop(0, NDIR, sources, 0)


def interact_pallas(columns, coupling, quad_offsets):
    comps, points = columns.shape
    spectra = columns.reshape(NFREQ, NDIR, points).transpose(1, 0, 2)
    freq_index = lax.iota(jnp.int32, NFREQ)
    inside = ((freq_index + quad_offsets[0] < NFREQ) & (freq_index - quad_offsets[1] >= 0)).astype(jnp.float32)
    weight = (coupling * inside)[:, None]
    out = pl.pallas_call(
        interact_kernel,
        out_shape=jax.ShapeDtypeStruct((NDIR, NFREQ, points), jnp.float32),
        in_specs=[
            pl.BlockSpec(memory_space=pltpu.SMEM),
            pl.BlockSpec(memory_space=pltpu.VMEM),
            pl.BlockSpec(memory_space=pltpu.VMEM),
        ],
        out_specs=pl.BlockSpec(memory_space=pltpu.VMEM),
        scratch_shapes=[pltpu.VMEM((2, NDIR, NFREQ, points), jnp.float32)],
    )(quad_offsets, weight, spectra)
    return out.transpose(1, 0, 2).reshape(comps, points)


def per_component(lookup, freq_index):
    matches = freq_index[:, None] == lax.iota(jnp.int32, lookup.shape[0])[None, :]
    return jnp.sum(jnp.where(matches, lookup[None, :], 0.0), axis=1)


def propagate(energy, ext_mask, courant_y, courant_x):
    for substep in range(SUBSTEPS):
        energy = quickest(energy, courant_y, 1)
        ext_mask = cut_slab(ext_mask, 2, ext_mask.shape[0] - 4, 0)
        energy = quickest_x(energy, courant_x) * ext_mask
    return energy


def on_device(spectrum, transparency, sea_order, speeds, sprinkle, coupling, quad_offsets):
    local_comps = spectrum.shape[0]
    band_rows = spectrum.shape[1]
    first_comp = lax.axis_index("spec") * local_comps
    comp_index = first_comp + lax.iota(jnp.int32, local_comps)
    freq_index = comp_index // NDIR
    dir_index = comp_index % NDIR
    angles = 2.0 * math.pi * (dir_index.astype(jnp.float32) + 0.5) / NDIR
    sines = jnp.sin(angles)
    cosines = jnp.cos(angles)
    speed_comp = per_component(speeds, freq_index)
    spread = per_component(sprinkle, freq_index)
    courant_y = (speed_comp * sines)[:, None, None]
    courant_x = (speed_comp * cosines)[:, None, None]
    spread_y = (spread * (sines * sines + 0.25 * cosines * cosines))[:, None, None]
    spread_x = (spread * (cosines * cosines + 0.25 * sines * sines))[:, None, None]
    width = 2 * SUBSTEPS + 2
    split = local_comps // 2 if local_comps % 2 == 0 else local_comps
    parts = [
        jnp.concatenate([transparency[None], spectrum[start : start + split]], axis=0)
        for start in range(0, local_comps, split)
    ]
    borders = [border_rows(part, "lat", 1, width) for part in parts]
    pieces = []
    start = 0
    for part, (low, high) in zip(parts, borders):
        if pieces:
            pieces[-1], low, high = lax.optimization_barrier((pieces[-1], low, high))
        part = jnp.concatenate([low, part, high], axis=1)
        stop = start + part.shape[0] - 1
        with_rim = propagate(part[1:], part[0], courant_y[start:stop], courant_x[start:stop])
        centre = cut_slab(with_rim, 2, band_rows, 1)
        pieces.append(
            (
                centre
                + spread_y[start:stop] * laplace(with_rim, 1)
                + spread_x[start:stop] * laplace_x(centre)
            )
            * transparency
        )
        start = stop
    smoothed = jnp.concatenate(pieces, axis=0)
    flat_cells = smoothed.reshape(local_comps, -1)
    sea_cells = sea_order.reshape(-1)[:SEA_MAX]
    columns = flat_cells.at[:, sea_cells].get(mode="promise_in_bounds", unique_indices=True)
    gathered = lax.all_to_all(columns, "spec", split_axis=1, concat_axis=0, tiled=True)
    source_terms = interact_pallas(gathered, coupling, quad_offsets)
    returned = lax.all_to_all(source_terms, "spec", split_axis=0, concat_axis=1, tiled=True)
    new_cells = flat_cells.at[:, sea_cells].add(
        returned, mode="promise_in_bounds", unique_indices=True
    )
    updated = new_cells.reshape(smoothed.shape)
    return (updated, source_terms.astype(jnp.bfloat16)[None])


def solution(mesh):
    in_specs = (
        P("spec", "lat", "groups"),
        P("lat", "groups"),
        P("lat", "groups"),
        P(),
        P(),
        P(),
        P(),
    )
    out_specs = (P("spec", "lat", "groups"), P(("groups", "lat"), None, "spec"))
    return jax.shard_map(
        on_device, mesh=mesh, in_specs=in_specs, out_specs=out_specs, check_vma=False
    )
```

```python
import math

import jax
import jax.numpy as jnp
from jax import lax
from jax.experimental import pallas as pl
from jax.experimental.pallas import tpu as pltpu
from jax.sharding import PartitionSpec as P

NDIR = 36
NFREQ = 32
SUBSTEPS = 2
SEA_MAX = 3072


gain_up = 1.25 ** (-4)
gain_down = 0.75 ** (-4)
gain_cross = 0.9375 ** (-4)


def border_rows(block, axis, dim, width):
    count = lax.axis_size(axis)
    bottom = lax.slice_in_dim(block, block.shape[dim] - width, None, axis=dim)
    top = lax.slice_in_dim(block, 0, width, axis=dim)
    if count == 2:
        first = lax.axis_index(axis) == 0
        swapped = lax.ppermute(jnp.where(first, bottom, top), axis, [(0, 1), (1, 0)])
        return jnp.where(first, 0.0, swapped), jnp.where(first, swapped, 0.0)
    forward = [(i, i + 1) for i in range(count - 1)]
    backward = [(target, source) for source, target in forward]
    return lax.ppermute(bottom, axis, forward), lax.ppermute(top, axis, backward)


def cut_slab(values, offset, length, along):
    return lax.slice_in_dim(values, offset, offset + length, axis=along)


def quickest(padded, courant, along):
    length = padded.shape[along] - 4
    before_cell = cut_slab(padded, 0, length + 1, along)
    left_cell = cut_slab(padded, 1, length + 1, along)
    right_cell = cut_slab(padded, 2, length + 1, along)
    after_cell = cut_slab(padded, 3, length + 1, along)
    curvature = jnp.where(
        courant > 0,
        right_cell - 2.0 * left_cell + before_cell,
        after_cell - 2.0 * right_cell + left_cell,
    )
    face_value = (
        0.5 * (left_cell + right_cell)
        - 0.5 * courant * (right_cell - left_cell)
        - (1.0 - courant * courant) / 6.0 * curvature
    )
    face_flux = courant * face_value
    return cut_slab(padded, 2, length, along) - (
        cut_slab(face_flux, 1, length, along) - cut_slab(face_flux, 0, length, along)
    )


def shifted(values, offset, along):
    config = [(0, 0, 0)] * values.ndim
    config[along] = (offset, -offset, 0)
    return lax.pad(values, jnp.zeros((), values.dtype), config)


def face_flux(before_cell, left_cell, right_cell, after_cell, courant):
    curvature = jnp.where(
        courant > 0,
        right_cell - 2.0 * left_cell + before_cell,
        after_cell - 2.0 * right_cell + left_cell,
    )
    face_value = (
        0.5 * (left_cell + right_cell)
        - 0.5 * courant * (right_cell - left_cell)
        - (1.0 - courant * courant) / 6.0 * curvature
    )
    return courant * face_value


def quickest_x(energy, courant):
    back_two = shifted(energy, 2, 2)
    back_one = shifted(energy, 1, 2)
    ahead_one = shifted(energy, -1, 2)
    ahead_two = shifted(energy, -2, 2)
    right_face = face_flux(back_one, energy, ahead_one, ahead_two, courant)
    left_face = face_flux(back_two, back_one, energy, ahead_one, courant)
    return energy - (right_face - left_face)


def laplace_x(centre):
    near_sum = shifted(centre, 1, 2) + shifted(centre, -1, 2) - 2.0 * centre
    far_sum = shifted(centre, 2, 2) + shifted(centre, -2, 2) - 2.0 * centre
    return 4.0 / 3.0 * near_sum - 1.0 / 12.0 * far_sum


def laplace(padded, along):
    length = padded.shape[along] - 4
    centre = cut_slab(padded, 2, length, along)
    near_sum = (
        cut_slab(padded, 1, length, along) + cut_slab(padded, 3, length, along) - 2.0 * centre
    )
    far_sum = cut_slab(padded, 0, length, along) + cut_slab(padded, 4, length, along) - 2.0 * centre
    return 4.0 / 3.0 * near_sum - 1.0 / 12.0 * far_sum


def interact_kernel(off_ref, w_ref, e_ref, s_ref, t_ref):
    up_freq = off_ref[0]
    down_freq = off_ref[1]
    dir_one = off_ref[2]
    dir_two = off_ref[3]
    weight = w_ref[...]
    up_shift = (NFREQ - up_freq) % NFREQ
    down_shift = down_freq % NFREQ

    def transfers(d, carry):
        spectra = e_ref[d]
        squared = spectra * spectra
        for slot, mirror in enumerate((1, -1)):
            upper_bin = pltpu.roll(e_ref[(d + mirror * dir_one) % NDIR], up_shift, 0)
            lower_bin = pltpu.roll(e_ref[(d - mirror * dir_two) % NDIR], down_shift, 0)
            t_ref[slot, d] = weight * (
                squared * (upper_bin * gain_up + lower_bin * gain_down)
                - 2.0 * gain_cross * spectra * upper_bin * lower_bin
            )
        return carry

    lax.fori_loop(0, NDIR, transfers, 0)

    def sources(d, carry):
        total = -2.0 * t_ref[0, d] - 2.0 * t_ref[1, d]
        for slot, mirror in enumerate((1, -1)):
            total = total + pltpu.roll(t_ref[slot, (d - mirror * dir_one) % NDIR], up_freq % NFREQ, 0)
            total = total + pltpu.roll(
                t_ref[slot, (d + mirror * dir_two) % NDIR], (NFREQ - down_freq) % NFREQ, 0
            )
        s_ref[d] = total
        return carry

    lax.fori_loop(0, NDIR, sources, 0)


def interact_pallas(columns, coupling, quad_offsets):
    comps, points = columns.shape
    spectra = columns.reshape(NFREQ, NDIR, points).transpose(1, 0, 2)
    freq_index = lax.iota(jnp.int32, NFREQ)
    inside = ((freq_index + quad_offsets[0] < NFREQ) & (freq_index - quad_offsets[1] >= 0)).astype(jnp.float32)
    weight = (coupling * inside)[:, None]
    out = pl.pallas_call(
        interact_kernel,
        out_shape=jax.ShapeDtypeStruct((NDIR, NFREQ, points), jnp.float32),
        in_specs=[
            pl.BlockSpec(memory_space=pltpu.SMEM),
            pl.BlockSpec(memory_space=pltpu.VMEM),
            pl.BlockSpec(memory_space=pltpu.VMEM),
        ],
        out_specs=pl.BlockSpec(memory_space=pltpu.VMEM),
        scratch_shapes=[pltpu.VMEM((2, NDIR, NFREQ, points), jnp.float32)],
    )(quad_offsets, weight, spectra)
    return out.transpose(1, 0, 2).reshape(comps, points)


def per_component(lookup, freq_index):
    matches = freq_index[:, None] == lax.iota(jnp.int32, lookup.shape[0])[None, :]
    return jnp.sum(jnp.where(matches, lookup[None, :], 0.0), axis=1)


def propagate(energy, ext_mask, courant_y, courant_x):
    for substep in range(SUBSTEPS):
        energy = quickest(energy, courant_y, 1)
        ext_mask = cut_slab(ext_mask, 2, ext_mask.shape[0] - 4, 0)
        energy = quickest_x(energy, courant_x) * ext_mask
    return energy


def on_device(spectrum, transparency, sea_order, speeds, sprinkle, coupling, quad_offsets):
    local_comps = spectrum.shape[0]
    band_rows = spectrum.shape[1]
    first_comp = lax.axis_index("spec") * local_comps
    comp_index = first_comp + lax.iota(jnp.int32, local_comps)
    freq_index = comp_index // NDIR
    dir_index = comp_index % NDIR
    angles = 2.0 * math.pi * (dir_index.astype(jnp.float32) + 0.5) / NDIR
    sines = jnp.sin(angles)
    cosines = jnp.cos(angles)
    speed_comp = per_component(speeds, freq_index)
    spread = per_component(sprinkle, freq_index)
    courant_y = (speed_comp * sines)[:, None, None]
    courant_x = (speed_comp * cosines)[:, None, None]
    spread_y = (spread * (sines * sines + 0.25 * cosines * cosines))[:, None, None]
    spread_x = (spread * (cosines * cosines + 0.25 * sines * sines))[:, None, None]
    stacked = jnp.concatenate([transparency[None], spectrum], axis=0)
    width = 2 * SUBSTEPS + 2

    def smooth_window(window):
        rows = window.shape[1] - 2 * width
        with_rim = propagate(window[1:], window[0], courant_y, courant_x)
        centre = cut_slab(with_rim, 2, rows, 1)
        return (
            centre + spread_y * laplace(with_rim, 1) + spread_x * laplace_x(centre)
        ) * cut_slab(window[0], width, rows, 0)

    low, high = border_rows(stacked, "lat", 1, width)
    if band_rows > 2 * width:
        inner = smooth_window(stacked)
        top = smooth_window(jnp.concatenate([low, stacked[:, : 2 * width]], axis=1))
        bottom = smooth_window(jnp.concatenate([stacked[:, band_rows - 2 * width :], high], axis=1))
        smoothed = jnp.concatenate([top, inner, bottom], axis=1)
    else:
        smoothed = smooth_window(jnp.concatenate([low, stacked, high], axis=1))
    flat_cells = smoothed.reshape(local_comps, -1)
    sea_cells = sea_order.reshape(-1)[:SEA_MAX]
    columns = flat_cells.at[:, sea_cells].get(mode="promise_in_bounds", unique_indices=True)
    gathered = lax.all_to_all(columns, "spec", split_axis=1, concat_axis=0, tiled=True)
    source_terms = interact_pallas(gathered, coupling, quad_offsets)
    returned = lax.all_to_all(source_terms, "spec", split_axis=0, concat_axis=1, tiled=True)
    new_cells = flat_cells.at[:, sea_cells].add(
        returned, mode="promise_in_bounds", unique_indices=True
    )
    updated = new_cells.reshape(smoothed.shape)
    return (updated, source_terms.astype(jnp.bfloat16)[None])


def solution(mesh):
    in_specs = (
        P("spec", "lat", "groups"),
        P("lat", "groups"),
        P("lat", "groups"),
        P(),
        P(),
        P(),
        P(),
    )
    out_specs = (P("spec", "lat", "groups"), P(("groups", "lat"), None, "spec"))
    return jax.shard_map(
        on_device, mesh=mesh, in_specs=in_specs, out_specs=out_specs, check_vma=False
    )
```

```python
import math

import jax
import jax.numpy as jnp
from jax import lax
from jax.experimental import pallas as pl
from jax.experimental.pallas import tpu as pltpu
from jax.sharding import PartitionSpec as P

NDIR = 36
NFREQ = 32
SUBSTEPS = 2
SEA_MAX = 3072


gain_up = 1.25 ** (-4)
gain_down = 0.75 ** (-4)
gain_cross = 0.9375 ** (-4)


def extended_2(block, sides, width):
    for axis, dim in sides:
        count = lax.axis_size(axis)
        bottom = lax.slice_in_dim(block, block.shape[dim] - width, None, axis=dim)
        top = lax.slice_in_dim(block, 0, width, axis=dim)
        if count == 2:
            first = lax.axis_index(axis) == 0
            swapped = lax.ppermute(jnp.where(first, bottom, top), axis, [(0, 1), (1, 0)])
            low = jnp.where(first, 0.0, swapped)
            high = jnp.where(first, swapped, 0.0)
        else:
            forward = [(i, i + 1) for i in range(count - 1)]
            backward = [(target, source) for source, target in forward]
            low = lax.ppermute(bottom, axis, forward)
            high = lax.ppermute(top, axis, backward)
        block = jnp.concatenate([low, block, high], axis=dim)
    return block


def cut_slab(values, offset, length, along):
    return lax.slice_in_dim(values, offset, offset + length, axis=along)


def quickest(padded, courant, along):
    length = padded.shape[along] - 4
    before_cell = cut_slab(padded, 0, length + 1, along)
    left_cell = cut_slab(padded, 1, length + 1, along)
    right_cell = cut_slab(padded, 2, length + 1, along)
    after_cell = cut_slab(padded, 3, length + 1, along)
    curvature = jnp.where(
        courant > 0,
        right_cell - 2.0 * left_cell + before_cell,
        after_cell - 2.0 * right_cell + left_cell,
    )
    face_value = (
        0.5 * (left_cell + right_cell)
        - 0.5 * courant * (right_cell - left_cell)
        - (1.0 - courant * courant) / 6.0 * curvature
    )
    face_flux = courant * face_value
    return cut_slab(padded, 2, length, along) - (
        cut_slab(face_flux, 1, length, along) - cut_slab(face_flux, 0, length, along)
    )


def shifted(values, offset, along):
    config = [(0, 0, 0)] * values.ndim
    config[along] = (offset, -offset, 0)
    return lax.pad(values, jnp.zeros((), values.dtype), config)


def face_flux(before_cell, left_cell, right_cell, after_cell, courant):
    curvature = jnp.where(
        courant > 0,
        right_cell - 2.0 * left_cell + before_cell,
        after_cell - 2.0 * right_cell + left_cell,
    )
    face_value = (
        0.5 * (left_cell + right_cell)
        - 0.5 * courant * (right_cell - left_cell)
        - (1.0 - courant * courant) / 6.0 * curvature
    )
    return courant * face_value


def quickest_x(energy, courant):
    back_two = shifted(energy, 2, 2)
    back_one = shifted(energy, 1, 2)
    ahead_one = shifted(energy, -1, 2)
    ahead_two = shifted(energy, -2, 2)
    right_face = face_flux(back_one, energy, ahead_one, ahead_two, courant)
    left_face = face_flux(back_two, back_one, energy, ahead_one, courant)
    return energy - (right_face - left_face)


def laplace_x(centre):
    near_sum = shifted(centre, 1, 2) + shifted(centre, -1, 2) - 2.0 * centre
    far_sum = shifted(centre, 2, 2) + shifted(centre, -2, 2) - 2.0 * centre
    return 4.0 / 3.0 * near_sum - 1.0 / 12.0 * far_sum


def laplace(padded, along):
    length = padded.shape[along] - 4
    centre = cut_slab(padded, 2, length, along)
    near_sum = (
        cut_slab(padded, 1, length, along) + cut_slab(padded, 3, length, along) - 2.0 * centre
    )
    far_sum = cut_slab(padded, 0, length, along) + cut_slab(padded, 4, length, along) - 2.0 * centre
    return 4.0 / 3.0 * near_sum - 1.0 / 12.0 * far_sum


def interact_kernel(off_ref, w_ref, e_ref, s_ref, t_ref):
    up_freq = off_ref[0]
    down_freq = off_ref[1]
    dir_one = off_ref[2]
    dir_two = off_ref[3]
    weight = w_ref[...]
    up_shift = (NFREQ - up_freq) % NFREQ
    down_shift = down_freq % NFREQ

    def transfers(d, carry):
        spectra = e_ref[d]
        squared = spectra * spectra
        for slot, mirror in enumerate((1, -1)):
            upper_bin = pltpu.roll(e_ref[(d + mirror * dir_one) % NDIR], up_shift, 0)
            lower_bin = pltpu.roll(e_ref[(d - mirror * dir_two) % NDIR], down_shift, 0)
            t_ref[slot, d] = weight * (
                squared * (upper_bin * gain_up + lower_bin * gain_down)
                - 2.0 * gain_cross * spectra * upper_bin * lower_bin
            )
        return carry

    lax.fori_loop(0, NDIR, transfers, 0)

    def sources(d, carry):
        total = -2.0 * t_ref[0, d] - 2.0 * t_ref[1, d]
        for slot, mirror in enumerate((1, -1)):
            total = total + pltpu.roll(t_ref[slot, (d - mirror * dir_one) % NDIR], up_freq % NFREQ, 0)
            total = total + pltpu.roll(
                t_ref[slot, (d + mirror * dir_two) % NDIR], (NFREQ - down_freq) % NFREQ, 0
            )
        s_ref[d] = total
        return carry

    lax.fori_loop(0, NDIR, sources, 0)


def interact_pallas(columns, coupling, quad_offsets):
    comps, points = columns.shape
    spectra = columns.reshape(NFREQ, NDIR, points).transpose(1, 0, 2)
    freq_index = lax.iota(jnp.int32, NFREQ)
    inside = ((freq_index + quad_offsets[0] < NFREQ) & (freq_index - quad_offsets[1] >= 0)).astype(jnp.float32)
    weight = (coupling * inside)[:, None]
    out = pl.pallas_call(
        interact_kernel,
        out_shape=jax.ShapeDtypeStruct((NDIR, NFREQ, points), jnp.float32),
        in_specs=[
            pl.BlockSpec(memory_space=pltpu.SMEM),
            pl.BlockSpec(memory_space=pltpu.VMEM),
            pl.BlockSpec(memory_space=pltpu.VMEM),
        ],
        out_specs=pl.BlockSpec(memory_space=pltpu.VMEM),
        scratch_shapes=[pltpu.VMEM((2, NDIR, NFREQ, points), jnp.float32)],
    )(quad_offsets, weight, spectra)
    return out.transpose(1, 0, 2).reshape(comps, points)


def per_component(lookup, freq_index):
    matches = freq_index[:, None] == lax.iota(jnp.int32, lookup.shape[0])[None, :]
    return jnp.sum(jnp.where(matches, lookup[None, :], 0.0), axis=1)


def propagate(energy, ext_mask, courant_y, courant_x):
    for substep in range(SUBSTEPS):
        energy = quickest(energy, courant_y, 1)
        ext_mask = cut_slab(ext_mask, 2, ext_mask.shape[0] - 4, 0)
        energy = quickest_x(energy, courant_x) * ext_mask
    return energy


def on_device(spectrum, transparency, sea_order, speeds, sprinkle, coupling, quad_offsets):
    local_comps = spectrum.shape[0]
    band_rows = spectrum.shape[1]
    first_comp = lax.axis_index("spec") * local_comps
    comp_index = first_comp + lax.iota(jnp.int32, local_comps)
    freq_index = comp_index // NDIR
    dir_index = comp_index % NDIR
    angles = 2.0 * math.pi * (dir_index.astype(jnp.float32) + 0.5) / NDIR
    sines = jnp.sin(angles)
    cosines = jnp.cos(angles)
    speed_comp = per_component(speeds, freq_index)
    spread = per_component(sprinkle, freq_index)
    courant_y = (speed_comp * sines)[:, None, None]
    courant_x = (speed_comp * cosines)[:, None, None]
    spread_y = (spread * (sines * sines + 0.25 * cosines * cosines))[:, None, None]
    spread_x = (spread * (cosines * cosines + 0.25 * sines * sines))[:, None, None]
    stacked = jnp.concatenate([transparency[None], spectrum], axis=0)
    reach = 2 * SUBSTEPS
    extended = extended_2(stacked, (("lat", 1),), reach + 2)
    with_rim = propagate(extended[1:], extended[0], courant_y, courant_x)
    centre = cut_slab(with_rim, 2, band_rows, 1)
    smoothed = (
        centre + spread_y * laplace(with_rim, 1) + spread_x * laplace_x(centre)
    ) * transparency
    flat_cells = smoothed.reshape(local_comps, -1)
    sea_cells = sea_order.reshape(-1)[:SEA_MAX]
    columns = flat_cells.at[:, sea_cells].get(mode="promise_in_bounds", unique_indices=True)
    gathered = lax.all_to_all(columns, "spec", split_axis=1, concat_axis=0, tiled=True)
    source_terms = interact_pallas(gathered, coupling, quad_offsets)
    returned = lax.all_to_all(source_terms, "spec", split_axis=0, concat_axis=1, tiled=True)
    order = sea_order.reshape(-1)
    slot_of_cell = jnp.zeros_like(order).at[order].set(
        lax.iota(jnp.int32, order.shape[0]), mode="promise_in_bounds", unique_indices=True
    )
    slot_terms = jnp.pad(returned, ((0, 0), (0, order.shape[0] - SEA_MAX)))
    cell_terms = slot_terms.at[:, slot_of_cell].get(mode="promise_in_bounds", unique_indices=True)
    updated = (flat_cells + cell_terms).reshape(smoothed.shape)
    return (updated, source_terms.astype(jnp.bfloat16)[None])


def solution(mesh):
    in_specs = (
        P("spec", "lat", "groups"),
        P("lat", "groups"),
        P("lat", "groups"),
        P(),
        P(),
        P(),
        P(),
    )
    out_specs = (P("spec", "lat", "groups"), P(("groups", "lat"), None, "spec"))
    return jax.shard_map(
        on_device, mesh=mesh, in_specs=in_specs, out_specs=out_specs, check_vma=False
    )
```

```python
import math

import jax
import jax.numpy as jnp
from jax import lax
from jax.experimental import pallas as pl
from jax.experimental.pallas import tpu as pltpu
from jax.sharding import PartitionSpec as P

NDIR = 36
NFREQ = 32
SUBSTEPS = 2
SEA_MAX = 3072


gain_up = 1.25 ** (-4)
gain_down = 0.75 ** (-4)
gain_cross = 0.9375 ** (-4)


def extended_2(block, sides, width):
    for axis, dim in sides:
        count = lax.axis_size(axis)
        bottom = lax.slice_in_dim(block, block.shape[dim] - width, None, axis=dim)
        top = lax.slice_in_dim(block, 0, width, axis=dim)
        if count == 2:
            first = lax.axis_index(axis) == 0
            swapped = lax.ppermute(jnp.where(first, bottom, top), axis, [(0, 1), (1, 0)])
            low = jnp.where(first, 0.0, swapped)
            high = jnp.where(first, swapped, 0.0)
        else:
            forward = [(i, i + 1) for i in range(count - 1)]
            backward = [(target, source) for source, target in forward]
            low = lax.ppermute(bottom, axis, forward)
            high = lax.ppermute(top, axis, backward)
        block = jnp.concatenate([low, block, high], axis=dim)
    return block


def cut_slab(values, offset, length, along):
    return lax.slice_in_dim(values, offset, offset + length, axis=along)


def quickest(padded, courant, along):
    length = padded.shape[along] - 4
    before_cell = cut_slab(padded, 0, length + 1, along)
    left_cell = cut_slab(padded, 1, length + 1, along)
    right_cell = cut_slab(padded, 2, length + 1, along)
    after_cell = cut_slab(padded, 3, length + 1, along)
    curvature = jnp.where(
        courant > 0,
        right_cell - 2.0 * left_cell + before_cell,
        after_cell - 2.0 * right_cell + left_cell,
    )
    face_value = (
        0.5 * (left_cell + right_cell)
        - 0.5 * courant * (right_cell - left_cell)
        - (1.0 - courant * courant) / 6.0 * curvature
    )
    face_flux = courant * face_value
    return cut_slab(padded, 2, length, along) - (
        cut_slab(face_flux, 1, length, along) - cut_slab(face_flux, 0, length, along)
    )


def shifted(values, offset, along):
    config = [(0, 0, 0)] * values.ndim
    config[along] = (offset, -offset, 0)
    return lax.pad(values, jnp.zeros((), values.dtype), config)


def face_flux(before_cell, left_cell, right_cell, after_cell, courant):
    curvature = jnp.where(
        courant > 0,
        right_cell - 2.0 * left_cell + before_cell,
        after_cell - 2.0 * right_cell + left_cell,
    )
    face_value = (
        0.5 * (left_cell + right_cell)
        - 0.5 * courant * (right_cell - left_cell)
        - (1.0 - courant * courant) / 6.0 * curvature
    )
    return courant * face_value


def quickest_x(energy, courant):
    back_two = shifted(energy, 2, 2)
    back_one = shifted(energy, 1, 2)
    ahead_one = shifted(energy, -1, 2)
    ahead_two = shifted(energy, -2, 2)
    right_face = face_flux(back_one, energy, ahead_one, ahead_two, courant)
    left_face = face_flux(back_two, back_one, energy, ahead_one, courant)
    return energy - (right_face - left_face)


def laplace_x(centre):
    near_sum = shifted(centre, 1, 2) + shifted(centre, -1, 2) - 2.0 * centre
    far_sum = shifted(centre, 2, 2) + shifted(centre, -2, 2) - 2.0 * centre
    return 4.0 / 3.0 * near_sum - 1.0 / 12.0 * far_sum


def laplace(padded, along):
    length = padded.shape[along] - 4
    centre = cut_slab(padded, 2, length, along)
    near_sum = (
        cut_slab(padded, 1, length, along) + cut_slab(padded, 3, length, along) - 2.0 * centre
    )
    far_sum = cut_slab(padded, 0, length, along) + cut_slab(padded, 4, length, along) - 2.0 * centre
    return 4.0 / 3.0 * near_sum - 1.0 / 12.0 * far_sum


def interact_kernel(off_ref, w_ref, e_ref, s_ref, t_ref):
    up_freq = off_ref[0]
    down_freq = off_ref[1]
    dir_one = off_ref[2]
    dir_two = off_ref[3]
    weight = w_ref[...]
    up_shift = (NFREQ - up_freq) % NFREQ
    down_shift = down_freq % NFREQ

    def transfers(d, carry):
        spectra = e_ref[d]
        squared = spectra * spectra
        for slot, mirror in enumerate((1, -1)):
            upper_bin = pltpu.roll(e_ref[(d + mirror * dir_one) % NDIR], up_shift, 0)
            lower_bin = pltpu.roll(e_ref[(d - mirror * dir_two) % NDIR], down_shift, 0)
            t_ref[slot, d] = weight * (
                squared * (upper_bin * gain_up + lower_bin * gain_down)
                - 2.0 * gain_cross * spectra * upper_bin * lower_bin
            )
        return carry

    lax.fori_loop(0, NDIR, transfers, 0)

    def sources(d, carry):
        total = -2.0 * t_ref[0, d] - 2.0 * t_ref[1, d]
        for slot, mirror in enumerate((1, -1)):
            total = total + pltpu.roll(t_ref[slot, (d - mirror * dir_one) % NDIR], up_freq % NFREQ, 0)
            total = total + pltpu.roll(
                t_ref[slot, (d + mirror * dir_two) % NDIR], (NFREQ - down_freq) % NFREQ, 0
            )
        s_ref[d] = total
        return carry

    lax.fori_loop(0, NDIR, sources, 0)


def interact_pallas(spectra, coupling, quad_offsets):
    freq_index = lax.iota(jnp.int32, NFREQ)
    inside = ((freq_index + quad_offsets[0] < NFREQ) & (freq_index - quad_offsets[1] >= 0)).astype(jnp.float32)
    weight = (coupling * inside)[:, None]
    return pl.pallas_call(
        interact_kernel,
        out_shape=jax.ShapeDtypeStruct(spectra.shape, jnp.float32),
        in_specs=[
            pl.BlockSpec(memory_space=pltpu.SMEM),
            pl.BlockSpec(memory_space=pltpu.VMEM),
            pl.BlockSpec(memory_space=pltpu.VMEM),
        ],
        out_specs=pl.BlockSpec(memory_space=pltpu.VMEM),
        scratch_shapes=[pltpu.VMEM((2,) + spectra.shape, jnp.float32)],
    )(quad_offsets, weight, spectra)


def per_component(lookup, freq_index):
    matches = freq_index[:, None] == lax.iota(jnp.int32, lookup.shape[0])[None, :]
    return jnp.sum(jnp.where(matches, lookup[None, :], 0.0), axis=1)


def propagate(energy, ext_mask, courant_y, courant_x):
    for substep in range(SUBSTEPS):
        energy = quickest(energy, courant_y, 1)
        ext_mask = cut_slab(ext_mask, 2, ext_mask.shape[0] - 4, 0)
        energy = quickest_x(energy, courant_x) * ext_mask
    return energy


def on_device(spectrum, transparency, sea_order, speeds, sprinkle, coupling, quad_offsets):
    local_comps = spectrum.shape[0]
    band_rows = spectrum.shape[1]
    first_comp = lax.axis_index("spec") * local_comps
    comp_index = first_comp + lax.iota(jnp.int32, local_comps)
    freq_index = comp_index // NDIR
    dir_index = comp_index % NDIR
    angles = 2.0 * math.pi * (dir_index.astype(jnp.float32) + 0.5) / NDIR
    sines = jnp.sin(angles)
    cosines = jnp.cos(angles)
    speed_comp = per_component(speeds, freq_index)
    spread = per_component(sprinkle, freq_index)
    courant_y = (speed_comp * sines)[:, None, None]
    courant_x = (speed_comp * cosines)[:, None, None]
    spread_y = (spread * (sines * sines + 0.25 * cosines * cosines))[:, None, None]
    spread_x = (spread * (cosines * cosines + 0.25 * sines * sines))[:, None, None]
    stacked = jnp.concatenate([transparency[None], spectrum], axis=0)
    reach = 2 * SUBSTEPS
    extended = extended_2(stacked, (("lat", 1),), reach + 2)
    with_rim = propagate(extended[1:], extended[0], courant_y, courant_x)
    centre = cut_slab(with_rim, 2, band_rows, 1)
    smoothed = (
        centre + spread_y * laplace(with_rim, 1) + spread_x * laplace_x(centre)
    ) * transparency
    cells_first = smoothed.reshape(local_comps, -1).T
    spec_size = lax.axis_size("spec")
    local_freqs = local_comps // NDIR
    sea_cells = sea_order.reshape(-1)[:SEA_MAX]
    points = SEA_MAX // spec_size
    rows = cells_first.at[sea_cells].get(mode="promise_in_bounds", unique_indices=True)
    gathered = lax.all_to_all(rows, "spec", split_axis=0, concat_axis=0, tiled=True)
    spectra = (
        gathered.reshape(spec_size, points, local_freqs, NDIR)
        .transpose(3, 0, 2, 1)
        .reshape(NDIR, NFREQ, points)
    )
    by_dir = interact_pallas(spectra, coupling, quad_offsets)
    source_terms = by_dir.transpose(1, 0, 2).reshape(NFREQ * NDIR, points)
    outgoing = (
        by_dir.reshape(NDIR, spec_size, local_freqs, points)
        .transpose(1, 3, 2, 0)
        .reshape(spec_size * points, local_comps)
    )
    returned = lax.all_to_all(outgoing, "spec", split_axis=0, concat_axis=0, tiled=True)
    new_cells = cells_first.at[sea_cells].add(
        returned, mode="promise_in_bounds", unique_indices=True
    )
    updated = new_cells.T.reshape(smoothed.shape)
    return (updated, source_terms.astype(jnp.bfloat16)[None])


def solution(mesh):
    in_specs = (
        P("spec", "lat", "groups"),
        P("lat", "groups"),
        P("lat", "groups"),
        P(),
        P(),
        P(),
        P(),
    )
    out_specs = (P("spec", "lat", "groups"), P(("groups", "lat"), None, "spec"))
    return jax.shard_map(
        on_device, mesh=mesh, in_specs=in_specs, out_specs=out_specs, check_vma=False
    )
```

```python
import math

import jax
import jax.numpy as jnp
from jax import lax
from jax.experimental import pallas as pl
from jax.experimental.pallas import tpu as pltpu
from jax.sharding import PartitionSpec as P

NDIR = 36
NFREQ = 32
SUBSTEPS = 2
SEA_MAX = 3072


gain_up = 1.25 ** (-4)
gain_down = 0.75 ** (-4)
gain_cross = 0.9375 ** (-4)


def extended_2(block, sides, width):
    for axis, dim in sides:
        count = lax.axis_size(axis)
        bottom = lax.slice_in_dim(block, block.shape[dim] - width, None, axis=dim)
        top = lax.slice_in_dim(block, 0, width, axis=dim)
        if count == 2:
            first = lax.axis_index(axis) == 0
            swapped = lax.ppermute(jnp.where(first, bottom, top), axis, [(0, 1), (1, 0)])
            low = jnp.where(first, 0.0, swapped)
            high = jnp.where(first, swapped, 0.0)
        else:
            forward = [(i, i + 1) for i in range(count - 1)]
            backward = [(target, source) for source, target in forward]
            low = lax.ppermute(bottom, axis, forward)
            high = lax.ppermute(top, axis, backward)
        block = jnp.concatenate([low, block, high], axis=dim)
    return block


def cut_slab(values, offset, length, along):
    return lax.slice_in_dim(values, offset, offset + length, axis=along)


def quickest(padded, courant, along):
    length = padded.shape[along] - 4
    before_cell = cut_slab(padded, 0, length + 1, along)
    left_cell = cut_slab(padded, 1, length + 1, along)
    right_cell = cut_slab(padded, 2, length + 1, along)
    after_cell = cut_slab(padded, 3, length + 1, along)
    curvature = jnp.where(
        courant > 0,
        right_cell - 2.0 * left_cell + before_cell,
        after_cell - 2.0 * right_cell + left_cell,
    )
    face_value = (
        0.5 * (left_cell + right_cell)
        - 0.5 * courant * (right_cell - left_cell)
        - (1.0 - courant * courant) / 6.0 * curvature
    )
    face_flux = courant * face_value
    return cut_slab(padded, 2, length, along) - (
        cut_slab(face_flux, 1, length, along) - cut_slab(face_flux, 0, length, along)
    )


def shifted(values, offset, along):
    config = [(0, 0, 0)] * values.ndim
    config[along] = (offset, -offset, 0)
    return lax.pad(values, jnp.zeros((), values.dtype), config)


def face_flux(before_cell, left_cell, right_cell, after_cell, courant):
    curvature = jnp.where(
        courant > 0,
        right_cell - 2.0 * left_cell + before_cell,
        after_cell - 2.0 * right_cell + left_cell,
    )
    face_value = (
        0.5 * (left_cell + right_cell)
        - 0.5 * courant * (right_cell - left_cell)
        - (1.0 - courant * courant) / 6.0 * curvature
    )
    return courant * face_value


def quickest_x(energy, courant):
    back_two = shifted(energy, 2, 2)
    back_one = shifted(energy, 1, 2)
    ahead_one = shifted(energy, -1, 2)
    ahead_two = shifted(energy, -2, 2)
    right_face = face_flux(back_one, energy, ahead_one, ahead_two, courant)
    left_face = face_flux(back_two, back_one, energy, ahead_one, courant)
    return energy - (right_face - left_face)


def laplace_x(centre):
    near_sum = shifted(centre, 1, 2) + shifted(centre, -1, 2) - 2.0 * centre
    far_sum = shifted(centre, 2, 2) + shifted(centre, -2, 2) - 2.0 * centre
    return 4.0 / 3.0 * near_sum - 1.0 / 12.0 * far_sum


def laplace(padded, along):
    length = padded.shape[along] - 4
    centre = cut_slab(padded, 2, length, along)
    near_sum = (
        cut_slab(padded, 1, length, along) + cut_slab(padded, 3, length, along) - 2.0 * centre
    )
    far_sum = cut_slab(padded, 0, length, along) + cut_slab(padded, 4, length, along) - 2.0 * centre
    return 4.0 / 3.0 * near_sum - 1.0 / 12.0 * far_sum


def interact_kernel(off_ref, w_ref, e_ref, s_ref, t_ref):
    up_freq = off_ref[0]
    down_freq = off_ref[1]
    dir_one = off_ref[2]
    dir_two = off_ref[3]
    weight = w_ref[...]
    up_shift = (NFREQ - up_freq) % NFREQ
    down_shift = down_freq % NFREQ

    def transfers(d, carry):
        spectra = e_ref[d]
        squared = spectra * spectra
        for slot, mirror in enumerate((1, -1)):
            upper_bin = pltpu.roll(e_ref[(d + mirror * dir_one) % NDIR], up_shift, 0)
            lower_bin = pltpu.roll(e_ref[(d - mirror * dir_two) % NDIR], down_shift, 0)
            t_ref[slot, d] = weight * (
                squared * (upper_bin * gain_up + lower_bin * gain_down)
                - 2.0 * gain_cross * spectra * upper_bin * lower_bin
            )
        return carry

    lax.fori_loop(0, NDIR, transfers, 0)

    def sources(d, carry):
        total = -2.0 * t_ref[0, d] - 2.0 * t_ref[1, d]
        for slot, mirror in enumerate((1, -1)):
            total = total + pltpu.roll(t_ref[slot, (d - mirror * dir_one) % NDIR], up_freq % NFREQ, 0)
            total = total + pltpu.roll(
                t_ref[slot, (d + mirror * dir_two) % NDIR], (NFREQ - down_freq) % NFREQ, 0
            )
        s_ref[d] = total
        return carry

    lax.fori_loop(0, NDIR, sources, 0)


def interact_pallas(spectra, coupling, quad_offsets):
    freq_index = lax.iota(jnp.int32, NFREQ)
    inside = ((freq_index + quad_offsets[0] < NFREQ) & (freq_index - quad_offsets[1] >= 0)).astype(jnp.float32)
    weight = (coupling * inside)[:, None]
    return pl.pallas_call(
        interact_kernel,
        out_shape=jax.ShapeDtypeStruct(spectra.shape, jnp.float32),
        in_specs=[
            pl.BlockSpec(memory_space=pltpu.SMEM),
            pl.BlockSpec(memory_space=pltpu.VMEM),
            pl.BlockSpec(memory_space=pltpu.VMEM),
        ],
        out_specs=pl.BlockSpec(memory_space=pltpu.VMEM),
        scratch_shapes=[pltpu.VMEM((2,) + spectra.shape, jnp.float32)],
    )(quad_offsets, weight, spectra)


def per_component(lookup, freq_index):
    matches = freq_index[:, None] == lax.iota(jnp.int32, lookup.shape[0])[None, :]
    return jnp.sum(jnp.where(matches, lookup[None, :], 0.0), axis=1)


def propagate(energy, ext_mask, courant_y, courant_x):
    for substep in range(SUBSTEPS):
        energy = quickest(energy, courant_y, 1)
        ext_mask = cut_slab(ext_mask, 2, ext_mask.shape[0] - 4, 0)
        energy = quickest_x(energy, courant_x) * ext_mask
    return energy


def on_device(spectrum, transparency, sea_order, speeds, sprinkle, coupling, quad_offsets):
    local_comps = spectrum.shape[0]
    band_rows = spectrum.shape[1]
    first_comp = lax.axis_index("spec") * local_comps
    comp_index = first_comp + lax.iota(jnp.int32, local_comps)
    freq_index = comp_index // NDIR
    dir_index = comp_index % NDIR
    angles = 2.0 * math.pi * (dir_index.astype(jnp.float32) + 0.5) / NDIR
    sines = jnp.sin(angles)
    cosines = jnp.cos(angles)
    speed_comp = per_component(speeds, freq_index)
    spread = per_component(sprinkle, freq_index)
    courant_y = (speed_comp * sines)[:, None, None]
    courant_x = (speed_comp * cosines)[:, None, None]
    spread_y = (spread * (sines * sines + 0.25 * cosines * cosines))[:, None, None]
    spread_x = (spread * (cosines * cosines + 0.25 * sines * sines))[:, None, None]
    stacked = jnp.concatenate([transparency[None], spectrum], axis=0)
    reach = 2 * SUBSTEPS
    extended = extended_2(stacked, (("lat", 1),), reach + 2)
    with_rim = propagate(extended[1:], extended[0], courant_y, courant_x)
    centre = cut_slab(with_rim, 2, band_rows, 1)
    smoothed = (
        centre + spread_y * laplace(with_rim, 1) + spread_x * laplace_x(centre)
    ) * transparency
    cells_first = smoothed.reshape(local_comps, -1).T
    spec_size = lax.axis_size("spec")
    local_freqs = local_comps // NDIR
    sea_cells = sea_order.reshape(-1)[:SEA_MAX]
    points = SEA_MAX // spec_size
    rows = cells_first.at[sea_cells].get(mode="promise_in_bounds", unique_indices=True)
    gathered = lax.all_to_all(rows, "spec", split_axis=0, concat_axis=0, tiled=True)
    spectra = (
        gathered.reshape(spec_size, points, local_freqs, NDIR)
        .transpose(3, 0, 2, 1)
        .reshape(NDIR, NFREQ, points)
    )
    by_dir = interact_pallas(spectra, coupling, quad_offsets)
    source_terms = by_dir.transpose(1, 0, 2).reshape(NFREQ * NDIR, points)
    outgoing = (
        by_dir.reshape(NDIR, spec_size, local_freqs, points)
        .transpose(1, 3, 2, 0)
        .reshape(spec_size * points, local_comps)
    )
    returned = lax.all_to_all(outgoing, "spec", split_axis=0, concat_axis=0, tiled=True)
    placed = jnp.zeros_like(cells_first).at[sea_cells].set(
        returned, mode="promise_in_bounds", unique_indices=True
    )
    updated = smoothed + placed.T.reshape(smoothed.shape)
    return (updated, source_terms.astype(jnp.bfloat16)[None])


def solution(mesh):
    in_specs = (
        P("spec", "lat", "groups"),
        P("lat", "groups"),
        P("lat", "groups"),
        P(),
        P(),
        P(),
        P(),
    )
    out_specs = (P("spec", "lat", "groups"), P(("groups", "lat"), None, "spec"))
    return jax.shard_map(
        on_device, mesh=mesh, in_specs=in_specs, out_specs=out_specs, check_vma=False
    )
```

```python
import math

import jax
import jax.numpy as jnp
from jax import lax
from jax.experimental import pallas as pl
from jax.experimental.pallas import tpu as pltpu
from jax.sharding import PartitionSpec as P

NDIR = 36
NFREQ = 32
SUBSTEPS = 2
SEA_MAX = 3072


gain_up = 1.25 ** (-4)
gain_down = 0.75 ** (-4)
gain_cross = 0.9375 ** (-4)


def extended_2(block, sides, width):
    for axis, dim in sides:
        count = lax.axis_size(axis)
        bottom = lax.slice_in_dim(block, block.shape[dim] - width, None, axis=dim)
        top = lax.slice_in_dim(block, 0, width, axis=dim)
        if count == 2:
            first = lax.axis_index(axis) == 0
            swapped = lax.ppermute(jnp.where(first, bottom, top), axis, [(0, 1), (1, 0)])
            low = jnp.where(first, 0.0, swapped)
            high = jnp.where(first, swapped, 0.0)
        else:
            forward = [(i, i + 1) for i in range(count - 1)]
            backward = [(target, source) for source, target in forward]
            low = lax.ppermute(bottom, axis, forward)
            high = lax.ppermute(top, axis, backward)
        block = jnp.concatenate([low, block, high], axis=dim)
    return block


def cut_slab(values, offset, length, along):
    return lax.slice_in_dim(values, offset, offset + length, axis=along)


def quickest(padded, courant, along):
    length = padded.shape[along] - 4
    before_cell = cut_slab(padded, 0, length + 1, along)
    left_cell = cut_slab(padded, 1, length + 1, along)
    right_cell = cut_slab(padded, 2, length + 1, along)
    after_cell = cut_slab(padded, 3, length + 1, along)
    curvature = jnp.where(
        courant > 0,
        right_cell - 2.0 * left_cell + before_cell,
        after_cell - 2.0 * right_cell + left_cell,
    )
    face_value = (
        0.5 * (left_cell + right_cell)
        - 0.5 * courant * (right_cell - left_cell)
        - (1.0 - courant * courant) / 6.0 * curvature
    )
    face_flux = courant * face_value
    return cut_slab(padded, 2, length, along) - (
        cut_slab(face_flux, 1, length, along) - cut_slab(face_flux, 0, length, along)
    )


def shifted(values, offset, along):
    config = [(0, 0, 0)] * values.ndim
    config[along] = (offset, -offset, 0)
    return lax.pad(values, jnp.zeros((), values.dtype), config)


def face_flux(before_cell, left_cell, right_cell, after_cell, courant):
    curvature = jnp.where(
        courant > 0,
        right_cell - 2.0 * left_cell + before_cell,
        after_cell - 2.0 * right_cell + left_cell,
    )
    face_value = (
        0.5 * (left_cell + right_cell)
        - 0.5 * courant * (right_cell - left_cell)
        - (1.0 - courant * courant) / 6.0 * curvature
    )
    return courant * face_value


def quickest_x(energy, courant):
    back_two = shifted(energy, 2, 2)
    back_one = shifted(energy, 1, 2)
    ahead_one = shifted(energy, -1, 2)
    ahead_two = shifted(energy, -2, 2)
    right_face = face_flux(back_one, energy, ahead_one, ahead_two, courant)
    left_face = face_flux(back_two, back_one, energy, ahead_one, courant)
    return energy - (right_face - left_face)


def laplace_x(centre):
    near_sum = shifted(centre, 1, 2) + shifted(centre, -1, 2) - 2.0 * centre
    far_sum = shifted(centre, 2, 2) + shifted(centre, -2, 2) - 2.0 * centre
    return 4.0 / 3.0 * near_sum - 1.0 / 12.0 * far_sum


def laplace(padded, along):
    length = padded.shape[along] - 4
    centre = cut_slab(padded, 2, length, along)
    near_sum = (
        cut_slab(padded, 1, length, along) + cut_slab(padded, 3, length, along) - 2.0 * centre
    )
    far_sum = cut_slab(padded, 0, length, along) + cut_slab(padded, 4, length, along) - 2.0 * centre
    return 4.0 / 3.0 * near_sum - 1.0 / 12.0 * far_sum


def interact_kernel(off_ref, w_ref, e_ref, s_ref, t_ref):
    up_freq = off_ref[0]
    down_freq = off_ref[1]
    dir_one = off_ref[2]
    dir_two = off_ref[3]
    weight = w_ref[...]
    up_shift = (NFREQ - up_freq) % NFREQ
    down_shift = down_freq % NFREQ

    def transfers(d, carry):
        spectra = e_ref[d]
        squared = spectra * spectra
        for slot, mirror in enumerate((1, -1)):
            upper_bin = pltpu.roll(e_ref[(d + mirror * dir_one) % NDIR], up_shift, 0)
            lower_bin = pltpu.roll(e_ref[(d - mirror * dir_two) % NDIR], down_shift, 0)
            t_ref[slot, d] = weight * (
                squared * (upper_bin * gain_up + lower_bin * gain_down)
                - 2.0 * gain_cross * spectra * upper_bin * lower_bin
            )
        return carry

    lax.fori_loop(0, NDIR, transfers, 0)

    def sources(d, carry):
        total = -2.0 * t_ref[0, d] - 2.0 * t_ref[1, d]
        for slot, mirror in enumerate((1, -1)):
            total = total + pltpu.roll(t_ref[slot, (d - mirror * dir_one) % NDIR], up_freq % NFREQ, 0)
            total = total + pltpu.roll(
                t_ref[slot, (d + mirror * dir_two) % NDIR], (NFREQ - down_freq) % NFREQ, 0
            )
        s_ref[d] = total
        return carry

    lax.fori_loop(0, NDIR, sources, 0)


def interact_pallas(spectra, coupling, quad_offsets):
    freq_index = lax.iota(jnp.int32, NFREQ)
    inside = ((freq_index + quad_offsets[0] < NFREQ) & (freq_index - quad_offsets[1] >= 0)).astype(jnp.float32)
    weight = (coupling * inside)[:, None]
    points = spectra.shape[2]
    block = 128 if points % 128 == 0 else points
    window = (NDIR, NFREQ, block)
    return pl.pallas_call(
        interact_kernel,
        out_shape=jax.ShapeDtypeStruct(spectra.shape, jnp.float32),
        grid=(points // block,),
        in_specs=[
            pl.BlockSpec(memory_space=pltpu.SMEM),
            pl.BlockSpec((NFREQ, 1), lambda i: (0, 0)),
            pl.BlockSpec(window, lambda i: (0, 0, i)),
        ],
        out_specs=pl.BlockSpec(window, lambda i: (0, 0, i)),
        scratch_shapes=[pltpu.VMEM((2,) + window, jnp.float32)],
    )(quad_offsets, weight, spectra)


def per_component(lookup, freq_index):
    matches = freq_index[:, None] == lax.iota(jnp.int32, lookup.shape[0])[None, :]
    return jnp.sum(jnp.where(matches, lookup[None, :], 0.0), axis=1)


def propagate(energy, ext_mask, courant_y, courant_x):
    for substep in range(SUBSTEPS):
        energy = quickest(energy, courant_y, 1)
        ext_mask = cut_slab(ext_mask, 2, ext_mask.shape[0] - 4, 0)
        energy = quickest_x(energy, courant_x) * ext_mask
    return energy


def on_device(spectrum, transparency, sea_order, speeds, sprinkle, coupling, quad_offsets):
    local_comps = spectrum.shape[0]
    band_rows = spectrum.shape[1]
    first_comp = lax.axis_index("spec") * local_comps
    comp_index = first_comp + lax.iota(jnp.int32, local_comps)
    freq_index = comp_index // NDIR
    dir_index = comp_index % NDIR
    angles = 2.0 * math.pi * (dir_index.astype(jnp.float32) + 0.5) / NDIR
    sines = jnp.sin(angles)
    cosines = jnp.cos(angles)
    speed_comp = per_component(speeds, freq_index)
    spread = per_component(sprinkle, freq_index)
    courant_y = (speed_comp * sines)[:, None, None]
    courant_x = (speed_comp * cosines)[:, None, None]
    spread_y = (spread * (sines * sines + 0.25 * cosines * cosines))[:, None, None]
    spread_x = (spread * (cosines * cosines + 0.25 * sines * sines))[:, None, None]
    stacked = jnp.concatenate([transparency[None], spectrum], axis=0)
    reach = 2 * SUBSTEPS
    extended = extended_2(stacked, (("lat", 1),), reach + 2)
    with_rim = propagate(extended[1:], extended[0], courant_y, courant_x)
    centre = cut_slab(with_rim, 2, band_rows, 1)
    smoothed = (
        centre + spread_y * laplace(with_rim, 1) + spread_x * laplace_x(centre)
    ) * transparency
    cells_first = smoothed.reshape(local_comps, -1).T
    spec_size = lax.axis_size("spec")
    local_freqs = local_comps // NDIR
    sea_cells = sea_order.reshape(-1)[:SEA_MAX]
    points = SEA_MAX // spec_size
    rows = cells_first.at[sea_cells].get(mode="promise_in_bounds", unique_indices=True)
    gathered = lax.all_to_all(rows, "spec", split_axis=0, concat_axis=0, tiled=True)
    spectra = (
        gathered.reshape(spec_size, points, local_freqs, NDIR)
        .transpose(3, 0, 2, 1)
        .reshape(NDIR, NFREQ, points)
    )
    by_dir = interact_pallas(spectra, coupling, quad_offsets)
    source_terms = by_dir.transpose(1, 0, 2).reshape(NFREQ * NDIR, points)
    outgoing = (
        by_dir.reshape(NDIR, spec_size, local_freqs, points)
        .transpose(1, 3, 2, 0)
        .reshape(spec_size * points, local_comps)
    )
    returned = lax.all_to_all(outgoing, "spec", split_axis=0, concat_axis=0, tiled=True)
    new_cells = cells_first.at[sea_cells].add(
        returned, mode="promise_in_bounds", unique_indices=True
    )
    updated = new_cells.T.reshape(smoothed.shape)
    return (updated, source_terms.astype(jnp.bfloat16)[None])


def solution(mesh):
    in_specs = (
        P("spec", "lat", "groups"),
        P("lat", "groups"),
        P("lat", "groups"),
        P(),
        P(),
        P(),
        P(),
    )
    out_specs = (P("spec", "lat", "groups"), P(("groups", "lat"), None, "spec"))
    return jax.shard_map(
        on_device, mesh=mesh, in_specs=in_specs, out_specs=out_specs, check_vma=False
    )
```

```python
import math

import jax
import jax.numpy as jnp
from jax import lax
from jax.experimental import pallas as pl
from jax.experimental.pallas import tpu as pltpu
from jax.sharding import PartitionSpec as P

NDIR = 36
NFREQ = 32
SUBSTEPS = 2
SEA_MAX = 3072


gain_up = 1.25 ** (-4)
gain_down = 0.75 ** (-4)
gain_cross = 0.9375 ** (-4)


def extended_2(block, sides, width):
    for axis, dim in sides:
        count = lax.axis_size(axis)
        bottom = lax.slice_in_dim(block, block.shape[dim] - width, None, axis=dim)
        top = lax.slice_in_dim(block, 0, width, axis=dim)
        if count == 2:
            first = lax.axis_index(axis) == 0
            swapped = lax.ppermute(jnp.where(first, bottom, top), axis, [(0, 1), (1, 0)])
            low = jnp.where(first, 0.0, swapped)
            high = jnp.where(first, swapped, 0.0)
        else:
            forward = [(i, i + 1) for i in range(count - 1)]
            backward = [(target, source) for source, target in forward]
            low = lax.ppermute(bottom, axis, forward)
            high = lax.ppermute(top, axis, backward)
        block = jnp.concatenate([low, block, high], axis=dim)
    return block


def cut_slab(values, offset, length, along):
    return lax.slice_in_dim(values, offset, offset + length, axis=along)


def quickest(padded, courant, along):
    length = padded.shape[along] - 4
    before_cell = cut_slab(padded, 0, length + 1, along)
    left_cell = cut_slab(padded, 1, length + 1, along)
    right_cell = cut_slab(padded, 2, length + 1, along)
    after_cell = cut_slab(padded, 3, length + 1, along)
    curvature = jnp.where(
        courant > 0,
        right_cell - 2.0 * left_cell + before_cell,
        after_cell - 2.0 * right_cell + left_cell,
    )
    face_value = (
        0.5 * (left_cell + right_cell)
        - 0.5 * courant * (right_cell - left_cell)
        - (1.0 - courant * courant) / 6.0 * curvature
    )
    face_flux = courant * face_value
    return cut_slab(padded, 2, length, along) - (
        cut_slab(face_flux, 1, length, along) - cut_slab(face_flux, 0, length, along)
    )


def shifted(values, offset, along):
    config = [(0, 0, 0)] * values.ndim
    config[along] = (offset, -offset, 0)
    return lax.pad(values, jnp.zeros((), values.dtype), config)


def face_flux(before_cell, left_cell, right_cell, after_cell, courant):
    curvature = jnp.where(
        courant > 0,
        right_cell - 2.0 * left_cell + before_cell,
        after_cell - 2.0 * right_cell + left_cell,
    )
    face_value = (
        0.5 * (left_cell + right_cell)
        - 0.5 * courant * (right_cell - left_cell)
        - (1.0 - courant * courant) / 6.0 * curvature
    )
    return courant * face_value


def quickest_x(energy, courant):
    back_two = shifted(energy, 2, 2)
    back_one = shifted(energy, 1, 2)
    ahead_one = shifted(energy, -1, 2)
    ahead_two = shifted(energy, -2, 2)
    right_face = face_flux(back_one, energy, ahead_one, ahead_two, courant)
    left_face = face_flux(back_two, back_one, energy, ahead_one, courant)
    return energy - (right_face - left_face)


def laplace_x(centre):
    near_sum = shifted(centre, 1, 2) + shifted(centre, -1, 2) - 2.0 * centre
    far_sum = shifted(centre, 2, 2) + shifted(centre, -2, 2) - 2.0 * centre
    return 4.0 / 3.0 * near_sum - 1.0 / 12.0 * far_sum


def laplace(padded, along):
    length = padded.shape[along] - 4
    centre = cut_slab(padded, 2, length, along)
    near_sum = (
        cut_slab(padded, 1, length, along) + cut_slab(padded, 3, length, along) - 2.0 * centre
    )
    far_sum = cut_slab(padded, 0, length, along) + cut_slab(padded, 4, length, along) - 2.0 * centre
    return 4.0 / 3.0 * near_sum - 1.0 / 12.0 * far_sum


def interact_kernel(off_ref, w_ref, e_ref, s_ref, t_ref):
    up_freq = off_ref[0]
    down_freq = off_ref[1]
    dir_one = off_ref[2]
    dir_two = off_ref[3]
    weight = w_ref[...]
    up_shift = (NFREQ - up_freq) % NFREQ
    down_shift = down_freq % NFREQ

    def transfers(d, carry):
        spectra = e_ref[d]
        squared = spectra * spectra
        for slot, mirror in enumerate((1, -1)):
            upper_bin = pltpu.roll(e_ref[(d + mirror * dir_one) % NDIR], up_shift, 0)
            lower_bin = pltpu.roll(e_ref[(d - mirror * dir_two) % NDIR], down_shift, 0)
            t_ref[slot, d] = weight * (
                squared * (upper_bin * gain_up + lower_bin * gain_down)
                - 2.0 * gain_cross * spectra * upper_bin * lower_bin
            )
        return carry

    lax.fori_loop(0, NDIR, transfers, 0, unroll=4)

    def sources(d, carry):
        total = -2.0 * t_ref[0, d] - 2.0 * t_ref[1, d]
        for slot, mirror in enumerate((1, -1)):
            total = total + pltpu.roll(t_ref[slot, (d - mirror * dir_one) % NDIR], up_freq % NFREQ, 0)
            total = total + pltpu.roll(
                t_ref[slot, (d + mirror * dir_two) % NDIR], (NFREQ - down_freq) % NFREQ, 0
            )
        s_ref[d] = total
        return carry

    lax.fori_loop(0, NDIR, sources, 0, unroll=4)


def interact_pallas(spectra, coupling, quad_offsets):
    freq_index = lax.iota(jnp.int32, NFREQ)
    inside = ((freq_index + quad_offsets[0] < NFREQ) & (freq_index - quad_offsets[1] >= 0)).astype(jnp.float32)
    weight = (coupling * inside)[:, None]
    return pl.pallas_call(
        interact_kernel,
        out_shape=jax.ShapeDtypeStruct(spectra.shape, jnp.float32),
        in_specs=[
            pl.BlockSpec(memory_space=pltpu.SMEM),
            pl.BlockSpec(memory_space=pltpu.VMEM),
            pl.BlockSpec(memory_space=pltpu.VMEM),
        ],
        out_specs=pl.BlockSpec(memory_space=pltpu.VMEM),
        scratch_shapes=[pltpu.VMEM((2,) + spectra.shape, jnp.float32)],
    )(quad_offsets, weight, spectra)


def per_component(lookup, freq_index):
    matches = freq_index[:, None] == lax.iota(jnp.int32, lookup.shape[0])[None, :]
    return jnp.sum(jnp.where(matches, lookup[None, :], 0.0), axis=1)


def propagate(energy, ext_mask, courant_y, courant_x):
    for substep in range(SUBSTEPS):
        energy = quickest(energy, courant_y, 1)
        ext_mask = cut_slab(ext_mask, 2, ext_mask.shape[0] - 4, 0)
        energy = quickest_x(energy, courant_x) * ext_mask
    return energy


def on_device(spectrum, transparency, sea_order, speeds, sprinkle, coupling, quad_offsets):
    local_comps = spectrum.shape[0]
    band_rows = spectrum.shape[1]
    first_comp = lax.axis_index("spec") * local_comps
    comp_index = first_comp + lax.iota(jnp.int32, local_comps)
    freq_index = comp_index // NDIR
    dir_index = comp_index % NDIR
    angles = 2.0 * math.pi * (dir_index.astype(jnp.float32) + 0.5) / NDIR
    sines = jnp.sin(angles)
    cosines = jnp.cos(angles)
    speed_comp = per_component(speeds, freq_index)
    spread = per_component(sprinkle, freq_index)
    courant_y = (speed_comp * sines)[:, None, None]
    courant_x = (speed_comp * cosines)[:, None, None]
    spread_y = (spread * (sines * sines + 0.25 * cosines * cosines))[:, None, None]
    spread_x = (spread * (cosines * cosines + 0.25 * sines * sines))[:, None, None]
    stacked = jnp.concatenate([transparency[None], spectrum], axis=0)
    reach = 2 * SUBSTEPS
    extended = extended_2(stacked, (("lat", 1),), reach + 2)
    with_rim = propagate(extended[1:], extended[0], courant_y, courant_x)
    centre = cut_slab(with_rim, 2, band_rows, 1)
    smoothed = (
        centre + spread_y * laplace(with_rim, 1) + spread_x * laplace_x(centre)
    ) * transparency
    cells_first = smoothed.reshape(local_comps, -1).T
    spec_size = lax.axis_size("spec")
    local_freqs = local_comps // NDIR
    sea_cells = sea_order.reshape(-1)[:SEA_MAX]
    points = SEA_MAX // spec_size
    rows = cells_first.at[sea_cells].get(mode="promise_in_bounds", unique_indices=True)
    gathered = lax.all_to_all(rows, "spec", split_axis=0, concat_axis=0, tiled=True)
    spectra = (
        gathered.reshape(spec_size, points, local_freqs, NDIR)
        .transpose(3, 0, 2, 1)
        .reshape(NDIR, NFREQ, points)
    )
    by_dir = interact_pallas(spectra, coupling, quad_offsets)
    source_terms = by_dir.astype(jnp.bfloat16).transpose(1, 0, 2).reshape(NFREQ * NDIR, points)
    outgoing = (
        by_dir.reshape(NDIR, spec_size, local_freqs, points)
        .transpose(1, 3, 2, 0)
        .reshape(spec_size * points, local_comps)
    )
    returned = lax.all_to_all(outgoing, "spec", split_axis=0, concat_axis=0, tiled=True)
    new_cells = cells_first.at[sea_cells].add(
        returned, mode="promise_in_bounds", unique_indices=True
    )
    updated = new_cells.T.reshape(smoothed.shape)
    return (updated, source_terms[None])


def solution(mesh):
    in_specs = (
        P("spec", "lat", "groups"),
        P("lat", "groups"),
        P("lat", "groups"),
        P(),
        P(),
        P(),
        P(),
    )
    out_specs = (P("spec", "lat", "groups"), P(("groups", "lat"), None, "spec"))
    return jax.shard_map(
        on_device, mesh=mesh, in_specs=in_specs, out_specs=out_specs, check_vma=False
    )
```

```python
import math

import jax
import jax.numpy as jnp
from jax import lax
from jax.experimental import pallas as pl
from jax.experimental.pallas import tpu as pltpu
from jax.sharding import PartitionSpec as P

NDIR = 36
NFREQ = 32
SUBSTEPS = 2
SEA_MAX = 3072


gain_up = 1.25 ** (-4)
gain_down = 0.75 ** (-4)
gain_cross = 0.9375 ** (-4)


def extended_2(block, sides, width):
    for axis, dim in sides:
        count = lax.axis_size(axis)
        bottom = lax.slice_in_dim(block, block.shape[dim] - width, None, axis=dim)
        top = lax.slice_in_dim(block, 0, width, axis=dim)
        if count == 2:
            first = lax.axis_index(axis) == 0
            swapped = lax.ppermute(jnp.where(first, bottom, top), axis, [(0, 1), (1, 0)])
            low = jnp.where(first, 0.0, swapped)
            high = jnp.where(first, swapped, 0.0)
        else:
            forward = [(i, i + 1) for i in range(count - 1)]
            backward = [(target, source) for source, target in forward]
            low = lax.ppermute(bottom, axis, forward)
            high = lax.ppermute(top, axis, backward)
        block = jnp.concatenate([low, block, high], axis=dim)
    return block


def cut_slab(values, offset, length, along):
    return lax.slice_in_dim(values, offset, offset + length, axis=along)


def quickest(padded, courant, along):
    length = padded.shape[along] - 4
    before_cell = cut_slab(padded, 0, length + 1, along)
    left_cell = cut_slab(padded, 1, length + 1, along)
    right_cell = cut_slab(padded, 2, length + 1, along)
    after_cell = cut_slab(padded, 3, length + 1, along)
    curvature = jnp.where(
        courant > 0,
        right_cell - 2.0 * left_cell + before_cell,
        after_cell - 2.0 * right_cell + left_cell,
    )
    face_value = (
        0.5 * (left_cell + right_cell)
        - 0.5 * courant * (right_cell - left_cell)
        - (1.0 - courant * courant) / 6.0 * curvature
    )
    face_flux = courant * face_value
    return cut_slab(padded, 2, length, along) - (
        cut_slab(face_flux, 1, length, along) - cut_slab(face_flux, 0, length, along)
    )


def shifted(values, offset, along):
    config = [(0, 0, 0)] * values.ndim
    config[along] = (offset, -offset, 0)
    return lax.pad(values, jnp.zeros((), values.dtype), config)


def face_flux(before_cell, left_cell, right_cell, after_cell, courant):
    curvature = jnp.where(
        courant > 0,
        right_cell - 2.0 * left_cell + before_cell,
        after_cell - 2.0 * right_cell + left_cell,
    )
    face_value = (
        0.5 * (left_cell + right_cell)
        - 0.5 * courant * (right_cell - left_cell)
        - (1.0 - courant * courant) / 6.0 * curvature
    )
    return courant * face_value


def quickest_x(energy, courant):
    back_two = shifted(energy, 2, 2)
    back_one = shifted(energy, 1, 2)
    ahead_one = shifted(energy, -1, 2)
    ahead_two = shifted(energy, -2, 2)
    right_face = face_flux(back_one, energy, ahead_one, ahead_two, courant)
    left_face = face_flux(back_two, back_one, energy, ahead_one, courant)
    return energy - (right_face - left_face)


def laplace_x(centre):
    near_sum = shifted(centre, 1, 2) + shifted(centre, -1, 2) - 2.0 * centre
    far_sum = shifted(centre, 2, 2) + shifted(centre, -2, 2) - 2.0 * centre
    return 4.0 / 3.0 * near_sum - 1.0 / 12.0 * far_sum


def laplace(padded, along):
    length = padded.shape[along] - 4
    centre = cut_slab(padded, 2, length, along)
    near_sum = (
        cut_slab(padded, 1, length, along) + cut_slab(padded, 3, length, along) - 2.0 * centre
    )
    far_sum = cut_slab(padded, 0, length, along) + cut_slab(padded, 4, length, along) - 2.0 * centre
    return 4.0 / 3.0 * near_sum - 1.0 / 12.0 * far_sum


def interact_kernel(off_ref, w_ref, e_ref, s_ref, t_ref):
    up_freq = off_ref[0]
    down_freq = off_ref[1]
    dir_one = off_ref[2]
    dir_two = off_ref[3]
    weight = w_ref[...]
    up_shift = (NFREQ - up_freq) % NFREQ
    down_shift = down_freq % NFREQ

    def transfers(d, carry):
        spectra = e_ref[d]
        squared = spectra * spectra
        for slot, mirror in enumerate((1, -1)):
            upper_bin = pltpu.roll(e_ref[(d + mirror * dir_one) % NDIR], up_shift, 0)
            lower_bin = pltpu.roll(e_ref[(d - mirror * dir_two) % NDIR], down_shift, 0)
            t_ref[slot, d] = weight * (
                squared * (upper_bin * gain_up + lower_bin * gain_down)
                - 2.0 * gain_cross * spectra * upper_bin * lower_bin
            )
        return carry

    lax.fori_loop(0, NDIR, transfers, 0, unroll=4)

    def sources(d, carry):
        total = -2.0 * t_ref[0, d] - 2.0 * t_ref[1, d]
        for slot, mirror in enumerate((1, -1)):
            total = total + pltpu.roll(t_ref[slot, (d - mirror * dir_one) % NDIR], up_freq % NFREQ, 0)
            total = total + pltpu.roll(
                t_ref[slot, (d + mirror * dir_two) % NDIR], (NFREQ - down_freq) % NFREQ, 0
            )
        s_ref[d] = total
        return carry

    lax.fori_loop(0, NDIR, sources, 0, unroll=4)


def interact_pallas(spectra, coupling, quad_offsets):
    freq_index = lax.iota(jnp.int32, NFREQ)
    inside = ((freq_index + quad_offsets[0] < NFREQ) & (freq_index - quad_offsets[1] >= 0)).astype(jnp.float32)
    weight = (coupling * inside)[:, None]
    return pl.pallas_call(
        interact_kernel,
        out_shape=jax.ShapeDtypeStruct(spectra.shape, jnp.float32),
        in_specs=[
            pl.BlockSpec(memory_space=pltpu.SMEM),
            pl.BlockSpec(memory_space=pltpu.VMEM),
            pl.BlockSpec(memory_space=pltpu.VMEM),
        ],
        out_specs=pl.BlockSpec(memory_space=pltpu.VMEM),
        scratch_shapes=[pltpu.VMEM((2,) + spectra.shape, jnp.float32)],
    )(quad_offsets, weight, spectra)


def per_component(lookup, freq_index):
    matches = freq_index[:, None] == lax.iota(jnp.int32, lookup.shape[0])[None, :]
    return jnp.sum(jnp.where(matches, lookup[None, :], 0.0), axis=1)


def propagate(energy, ext_mask, courant_y, courant_x):
    for substep in range(SUBSTEPS):
        energy = quickest(energy, courant_y, 1)
        ext_mask = cut_slab(ext_mask, 2, ext_mask.shape[0] - 4, 0)
        energy = quickest_x(energy, courant_x) * ext_mask
    return energy


def on_device(spectrum, transparency, sea_order, speeds, sprinkle, coupling, quad_offsets):
    local_comps = spectrum.shape[0]
    band_rows = spectrum.shape[1]
    first_comp = lax.axis_index("spec") * local_comps
    comp_index = first_comp + lax.iota(jnp.int32, local_comps)
    freq_index = comp_index // NDIR
    dir_index = comp_index % NDIR
    angles = 2.0 * math.pi * (dir_index.astype(jnp.float32) + 0.5) / NDIR
    sines = jnp.sin(angles)
    cosines = jnp.cos(angles)
    speed_comp = per_component(speeds, freq_index)
    spread = per_component(sprinkle, freq_index)
    courant_y = (speed_comp * sines)[:, None, None]
    courant_x = (speed_comp * cosines)[:, None, None]
    spread_y = (spread * (sines * sines + 0.25 * cosines * cosines))[:, None, None]
    spread_x = (spread * (cosines * cosines + 0.25 * sines * sines))[:, None, None]
    stacked = jnp.concatenate([transparency[None], spectrum], axis=0)
    reach = 2 * SUBSTEPS
    extended = extended_2(stacked, (("lat", 1),), reach + 2)
    with_rim = propagate(extended[1:], extended[0], courant_y, courant_x)
    centre = cut_slab(with_rim, 2, band_rows, 1)
    smoothed = (
        centre + spread_y * laplace(with_rim, 1) + spread_x * laplace_x(centre)
    ) * transparency
    cells_first = smoothed.reshape(local_comps, -1).T
    spec_size = lax.axis_size("spec")
    local_freqs = local_comps // NDIR
    sea_cells = sea_order.reshape(-1)[:SEA_MAX]
    points = SEA_MAX // spec_size
    rows = cells_first.at[sea_cells].get(mode="promise_in_bounds", unique_indices=True)
    gathered = lax.all_to_all(rows, "spec", split_axis=0, concat_axis=0, tiled=True)
    spectra = (
        gathered.reshape(spec_size, points, local_freqs, NDIR)
        .transpose(3, 0, 2, 1)
        .reshape(NDIR, NFREQ, points)
    )
    by_dir = interact_pallas(spectra, coupling, quad_offsets)
    source_terms = by_dir.astype(jnp.bfloat16).transpose(1, 0, 2).reshape(NFREQ * NDIR, points)
    outgoing = (
        by_dir.reshape(NDIR, spec_size, local_freqs, points)
        .transpose(1, 3, 2, 0)
        .reshape(spec_size * points, local_comps)
    )
    returned = lax.all_to_all(outgoing, "spec", split_axis=0, concat_axis=0, tiled=True)
    new_cells = cells_first.at[sea_cells].set(
        rows + returned, mode="promise_in_bounds", unique_indices=True
    )
    updated = new_cells.T.reshape(smoothed.shape)
    return (updated, source_terms[None])


def solution(mesh):
    in_specs = (
        P("spec", "lat", "groups"),
        P("lat", "groups"),
        P("lat", "groups"),
        P(),
        P(),
        P(),
        P(),
    )
    out_specs = (P("spec", "lat", "groups"), P(("groups", "lat"), None, "spec"))
    return jax.shard_map(
        on_device, mesh=mesh, in_specs=in_specs, out_specs=out_specs, check_vma=False
    )
```

```python
import math

import jax
import jax.numpy as jnp
from jax import lax
from jax.experimental import pallas as pl
from jax.experimental.pallas import tpu as pltpu
from jax.sharding import PartitionSpec as P

NDIR = 36
NFREQ = 32
SUBSTEPS = 2
SEA_MAX = 3072


gain_up = 1.25 ** (-4)
gain_down = 0.75 ** (-4)
gain_cross = 0.9375 ** (-4)


def extended_2(block, sides, width):
    for axis, dim in sides:
        count = lax.axis_size(axis)
        bottom = lax.slice_in_dim(block, block.shape[dim] - width, None, axis=dim)
        top = lax.slice_in_dim(block, 0, width, axis=dim)
        if count == 2:
            first = lax.axis_index(axis) == 0
            swapped = lax.ppermute(jnp.where(first, bottom, top), axis, [(0, 1), (1, 0)])
            low = jnp.where(first, 0.0, swapped)
            high = jnp.where(first, swapped, 0.0)
        else:
            forward = [(i, i + 1) for i in range(count - 1)]
            backward = [(target, source) for source, target in forward]
            low = lax.ppermute(bottom, axis, forward)
            high = lax.ppermute(top, axis, backward)
        block = jnp.concatenate([low, block, high], axis=dim)
    return block


def cut_slab(values, offset, length, along):
    return lax.slice_in_dim(values, offset, offset + length, axis=along)


def quickest(padded, courant, along):
    length = padded.shape[along] - 4
    before_cell = cut_slab(padded, 0, length + 1, along)
    left_cell = cut_slab(padded, 1, length + 1, along)
    right_cell = cut_slab(padded, 2, length + 1, along)
    after_cell = cut_slab(padded, 3, length + 1, along)
    curvature = jnp.where(
        courant > 0,
        right_cell - 2.0 * left_cell + before_cell,
        after_cell - 2.0 * right_cell + left_cell,
    )
    face_value = (
        0.5 * (left_cell + right_cell)
        - 0.5 * courant * (right_cell - left_cell)
        - (1.0 - courant * courant) / 6.0 * curvature
    )
    face_flux = courant * face_value
    return cut_slab(padded, 2, length, along) - (
        cut_slab(face_flux, 1, length, along) - cut_slab(face_flux, 0, length, along)
    )


def shifted(values, offset, along):
    config = [(0, 0, 0)] * values.ndim
    config[along] = (offset, -offset, 0)
    return lax.pad(values, jnp.zeros((), values.dtype), config)


def face_flux(before_cell, left_cell, right_cell, after_cell, courant):
    curvature = jnp.where(
        courant > 0,
        right_cell - 2.0 * left_cell + before_cell,
        after_cell - 2.0 * right_cell + left_cell,
    )
    face_value = (
        0.5 * (left_cell + right_cell)
        - 0.5 * courant * (right_cell - left_cell)
        - (1.0 - courant * courant) / 6.0 * curvature
    )
    return courant * face_value


def quickest_x(energy, courant):
    back_two = shifted(energy, 2, 2)
    back_one = shifted(energy, 1, 2)
    ahead_one = shifted(energy, -1, 2)
    ahead_two = shifted(energy, -2, 2)
    right_face = face_flux(back_one, energy, ahead_one, ahead_two, courant)
    left_face = face_flux(back_two, back_one, energy, ahead_one, courant)
    return energy - (right_face - left_face)


def laplace_x(centre):
    near_sum = shifted(centre, 1, 2) + shifted(centre, -1, 2) - 2.0 * centre
    far_sum = shifted(centre, 2, 2) + shifted(centre, -2, 2) - 2.0 * centre
    return 4.0 / 3.0 * near_sum - 1.0 / 12.0 * far_sum


def laplace(padded, along):
    length = padded.shape[along] - 4
    centre = cut_slab(padded, 2, length, along)
    near_sum = (
        cut_slab(padded, 1, length, along) + cut_slab(padded, 3, length, along) - 2.0 * centre
    )
    far_sum = cut_slab(padded, 0, length, along) + cut_slab(padded, 4, length, along) - 2.0 * centre
    return 4.0 / 3.0 * near_sum - 1.0 / 12.0 * far_sum


def interact_kernel(off_ref, w_ref, e_ref, s_ref, b_ref, t_ref):
    up_freq = off_ref[0]
    down_freq = off_ref[1]
    dir_one = off_ref[2]
    dir_two = off_ref[3]
    weight = w_ref[...]
    up_shift = (NFREQ - up_freq) % NFREQ
    down_shift = down_freq % NFREQ

    def transfers(d, carry):
        spectra = e_ref[d]
        squared = spectra * spectra
        for slot, mirror in enumerate((1, -1)):
            upper_bin = pltpu.roll(e_ref[(d + mirror * dir_one) % NDIR], up_shift, 0)
            lower_bin = pltpu.roll(e_ref[(d - mirror * dir_two) % NDIR], down_shift, 0)
            t_ref[slot, d] = weight * (
                squared * (upper_bin * gain_up + lower_bin * gain_down)
                - 2.0 * gain_cross * spectra * upper_bin * lower_bin
            )
        return carry

    lax.fori_loop(0, NDIR, transfers, 0, unroll=4)

    def sources(d, carry):
        total = -2.0 * t_ref[0, d] - 2.0 * t_ref[1, d]
        for slot, mirror in enumerate((1, -1)):
            total = total + pltpu.roll(t_ref[slot, (d - mirror * dir_one) % NDIR], up_freq % NFREQ, 0)
            total = total + pltpu.roll(
                t_ref[slot, (d + mirror * dir_two) % NDIR], (NFREQ - down_freq) % NFREQ, 0
            )
        s_ref[d] = total
        b_ref[d] = total.astype(jnp.bfloat16)
        return carry

    lax.fori_loop(0, NDIR, sources, 0, unroll=4)


def interact_pallas(spectra, coupling, quad_offsets):
    freq_index = lax.iota(jnp.int32, NFREQ)
    inside = ((freq_index + quad_offsets[0] < NFREQ) & (freq_index - quad_offsets[1] >= 0)).astype(jnp.float32)
    weight = (coupling * inside)[:, None]
    return pl.pallas_call(
        interact_kernel,
        out_shape=(
            jax.ShapeDtypeStruct(spectra.shape, jnp.float32),
            jax.ShapeDtypeStruct(spectra.shape, jnp.bfloat16),
        ),
        in_specs=[
            pl.BlockSpec(memory_space=pltpu.SMEM),
            pl.BlockSpec(memory_space=pltpu.VMEM),
            pl.BlockSpec(memory_space=pltpu.VMEM),
        ],
        out_specs=(
            pl.BlockSpec(memory_space=pltpu.VMEM),
            pl.BlockSpec(memory_space=pltpu.VMEM),
        ),
        scratch_shapes=[pltpu.VMEM((2,) + spectra.shape, jnp.float32)],
    )(quad_offsets, weight, spectra)


def per_component(lookup, freq_index):
    matches = freq_index[:, None] == lax.iota(jnp.int32, lookup.shape[0])[None, :]
    return jnp.sum(jnp.where(matches, lookup[None, :], 0.0), axis=1)


def propagate(energy, ext_mask, courant_y, courant_x):
    for substep in range(SUBSTEPS):
        energy = quickest(energy, courant_y, 1)
        ext_mask = cut_slab(ext_mask, 2, ext_mask.shape[0] - 4, 0)
        energy = quickest_x(energy, courant_x) * ext_mask
    return energy


def on_device(spectrum, transparency, sea_order, speeds, sprinkle, coupling, quad_offsets):
    local_comps = spectrum.shape[0]
    band_rows = spectrum.shape[1]
    first_comp = lax.axis_index("spec") * local_comps
    comp_index = first_comp + lax.iota(jnp.int32, local_comps)
    freq_index = comp_index // NDIR
    dir_index = comp_index % NDIR
    angles = 2.0 * math.pi * (dir_index.astype(jnp.float32) + 0.5) / NDIR
    sines = jnp.sin(angles)
    cosines = jnp.cos(angles)
    speed_comp = per_component(speeds, freq_index)
    spread = per_component(sprinkle, freq_index)
    courant_y = (speed_comp * sines)[:, None, None]
    courant_x = (speed_comp * cosines)[:, None, None]
    spread_y = (spread * (sines * sines + 0.25 * cosines * cosines))[:, None, None]
    spread_x = (spread * (cosines * cosines + 0.25 * sines * sines))[:, None, None]
    stacked = jnp.concatenate([transparency[None], spectrum], axis=0)
    reach = 2 * SUBSTEPS
    extended = extended_2(stacked, (("lat", 1),), reach + 2)
    with_rim = propagate(extended[1:], extended[0], courant_y, courant_x)
    centre = cut_slab(with_rim, 2, band_rows, 1)
    smoothed = (
        centre + spread_y * laplace(with_rim, 1) + spread_x * laplace_x(centre)
    ) * transparency
    cells_first = smoothed.reshape(local_comps, -1).T
    spec_size = lax.axis_size("spec")
    local_freqs = local_comps // NDIR
    sea_cells = sea_order.reshape(-1)[:SEA_MAX]
    points = SEA_MAX // spec_size
    rows = cells_first.at[sea_cells].get(mode="promise_in_bounds", unique_indices=True)
    gathered = lax.all_to_all(rows, "spec", split_axis=0, concat_axis=0, tiled=True)
    spectra = (
        gathered.reshape(spec_size, points, local_freqs, NDIR)
        .transpose(3, 0, 2, 1)
        .reshape(NDIR, NFREQ, points)
    )
    by_dir, rounded = interact_pallas(spectra, coupling, quad_offsets)
    source_terms = rounded.transpose(1, 0, 2).reshape(NFREQ * NDIR, points)
    outgoing = (
        by_dir.reshape(NDIR, spec_size, local_freqs, points)
        .transpose(1, 3, 2, 0)
        .reshape(spec_size * points, local_comps)
    )
    returned = lax.all_to_all(outgoing, "spec", split_axis=0, concat_axis=0, tiled=True)
    new_cells = cells_first.at[sea_cells].add(
        returned, mode="promise_in_bounds", unique_indices=True
    )
    updated = new_cells.T.reshape(smoothed.shape)
    return (updated, source_terms[None])


def solution(mesh):
    in_specs = (
        P("spec", "lat", "groups"),
        P("lat", "groups"),
        P("lat", "groups"),
        P(),
        P(),
        P(),
        P(),
    )
    out_specs = (P("spec", "lat", "groups"), P(("groups", "lat"), None, "spec"))
    return jax.shard_map(
        on_device, mesh=mesh, in_specs=in_specs, out_specs=out_specs, check_vma=False
    )
```
